256 devices in a mesh: pb: 4 (over x), item: 64 (over y, z, core).
Axes of the slice: x: 4, y: 4, z: 8, core: 2. Of those that a mesh axis runs over, the one named last changes fastest.
Arguments:
- questions: bfloat16 [2048, 1024], P(('pb', 'item')), may hold values from -500 to 500
- item_embeddings: bfloat16 [32768, 1024], P('item'), may hold values from -1.0546875 to 1.0546875
- block_ids: int32 [2048, 16], P(('pb', 'item')), may hold values from 0 to 255, all different within a row
- teacher_scores: bfloat16 [2048, 16, 128], P(('pb', 'item')), may hold values from -100 to 250
Outputs:
- loss: float32 [], replicated
- question_grads: float32 [2048, 1024], P(('pb', 'item'))
- item_grads: float32 [32768, 1024], P('item')
The draws below stay inside these ranges and needn't reach their ends.
Inputs may be any that keep to these rules, and one draw needn't show every extreme that they name: `block_ids`: the 16 block numbers of one question are all different, and every block is named by some question.
All inputs are finite; a program needn't handle non-finite values.
Results may differ from the reference program's by a relative error of at most 0.0049.
Values may be sent and summed in bfloat16 or wider, within the bound.
No kernel may reach another device: no remote copies, remote signals or barrier semaphores. Data moves between devices by JAX's collectives and lax.ppermute only.
A program may use at most 64 MiB of HBM per device.

```python
import jax
import jax.numpy as jnp
from jax import lax

D = 1024
BLK = 128
SLOTS = 16
NQ = 2048
NBLK = 256
NITEMS = 32768


def draw_questions(key, part):
    scale_base = D ** (-0.25)
    values = jnp.clip(jax.random.normal(key, (NQ, D), jnp.float32), -6.0, 6.0) * scale_base
    return values.astype(jnp.bfloat16)


def draw_teacher_scores(key, part):
    values = jnp.clip(jax.random.normal(key, (NQ, SLOTS, BLK), jnp.float32), -6.0, 6.0) * 3.0
    return values.astype(jnp.bfloat16)


def level_of(stream_key, extent, cuts, least, high):
    loudness = 1.0
    for dim, shards_of in cuts:
        steps = jax.random.uniform(jax.random.fold_in(jax.random.fold_in(stream_key, 6), dim), (shards_of,), jnp.float32, least / len(cuts), high / len(cuts))
        loudness = loudness * jnp.repeat(jnp.exp(steps), extent[dim] // shards_of).reshape((-1,) + (1,) * (len(extent) - 1 - dim))
    return loudness


def different_ones(own_key, rows, amount, top, lift):
    sequence = jax.random.permutation(jax.random.fold_in(own_key, 1), amount)
    favour = sequence
    for power in range(3):
        favour = favour * favour // amount
    favour = favour * lift // amount
    chance = jax.random.randint(jax.random.fold_in(own_key, 2), (rows, amount), 0, 4096) + favour
    holders = jax.random.permutation(jax.random.fold_in(own_key, 3), rows)[jnp.arange(amount) % rows]
    chance = jnp.where(jnp.arange(rows)[:, None] == holders[None, :], 1 << 14, chance)
    merit = chance * amount + jnp.arange(amount)
    return lax.top_k(merit.astype(jnp.int32), top)[1].astype(jnp.int32)


def normal_values(own_key, dims, width, most, split=(), kind=jnp.bfloat16):
    array = width * jax.random.normal(own_key, dims, jnp.float32)
    if split:
        array = array * level_of(own_key, dims, split, -0.22, 0.18)
    return jnp.clip(array, -most, most).astype(kind)


def setup_inputs(seed: int = 0) -> dict:
    key_list = jax.random.split(jax.random.key(seed), 5)
    return {
        "questions": draw_questions(jax.random.fold_in(key_list[4], 71), 0),
        "item_embeddings": normal_values(key_list[1], (NITEMS, D), (D ** -0.25), 1.0546875, ((0, 64),)),
        "block_ids": different_ones(key_list[2], NQ, NBLK, SLOTS, 1024),
        "teacher_scores": draw_teacher_scores(jax.random.fold_in(key_list[4], 71), 0),
    }


def row_lse(values):
    top = jnp.max(values, axis=1)
    return top + jnp.log(jnp.sum(jnp.exp(values - top[:, None]), axis=1))


def reference(questions, item_embeddings, block_ids, teacher_scores):
    table = item_embeddings.reshape(NBLK, BLK, D)
    group = 16
    qrows_all = questions.reshape(NQ // group, group, D)
    ids_all = block_ids.reshape(NQ // group, group, SLOTS)
    teach_all = teacher_scores.reshape(NQ // group, group, SLOTS, BLK)

    def step(carry, inputs):
        grads, total = carry
        qrows, ids, teach = inputs
        picked = jnp.take(table, ids, axis=0).astype(jnp.float32)
        qf = qrows.astype(jnp.float32)
        student = jnp.einsum('gd,gskd->gsk', qf, picked, precision=lax.Precision.HIGHEST)
        scores = student.reshape(group, SLOTS * BLK)
        teach_f = teach.astype(jnp.float32).reshape(group, SLOTS * BLK)
        lse_s = row_lse(scores)
        lse_t = row_lse(teach_f)
        probs = jnp.exp(scores - lse_s[:, None])
        target = jnp.exp(teach_f - lse_t[:, None])
        diverg = jnp.sum(target * (teach_f - scores), axis=1) - lse_t + lse_s
        coeff = (probs - target).astype(jnp.bfloat16).reshape(group, SLOTS, BLK).astype(jnp.float32)
        qgrad = jnp.einsum('gsk,gskd->gd', coeff, picked, precision=lax.Precision.HIGHEST)
        terms = jnp.einsum('gsk,gd->gskd', coeff, qf, precision=lax.Precision.HIGHEST)
        grads = grads.at[ids.reshape(-1)].add(terms.reshape(group * SLOTS, BLK, D))
        return (grads, total + jnp.sum(diverg)), qgrad

    start = (jnp.zeros((NBLK, BLK, D), jnp.float32), jnp.zeros((), jnp.float32))
    (grads, total), qgrads = lax.scan(step, start, (qrows_all, ids_all, teach_all))
    return (total / NQ, qgrads.reshape(NQ, D), grads.reshape(NITEMS, D))
```

```python
import jax
import jax.numpy as jnp
from jax import lax
from jax.sharding import PartitionSpec as P


def row_lse(values):
    top = jnp.max(values, axis=1)
    return top + jnp.log(jnp.sum(jnp.exp(values - top[:, None]), axis=1))


def shards(questions, item_embeddings, block_ids, teacher_scores):
    qdev, width = questions.shape
    slots = block_ids.shape[1]
    blk = teacher_scores.shape[2]
    own_items = item_embeddings.shape[0]
    blocks_here = own_items // blk
    nitem = lax.axis_size("item")
    panel = qdev * nitem
    cand = slots * blk
    base = lax.axis_index("item") * blocks_here

    packed = jnp.concatenate(
        [
            questions,
            teacher_scores.reshape(qdev, cand),
            block_ids.astype(jnp.bfloat16),
        ],
        axis=1,
    )
    gathered = lax.all_gather(packed, "item", axis=0, tiled=True)
    gathered_q = gathered[:, :width]
    teach_bf = gathered[:, width : width + cand]
    gathered_ids = gathered[:, width + cand :].astype(jnp.int32)

    teach_rows = teach_bf.astype(jnp.float32)
    lse_t = row_lse(teach_rows)

    scores = lax.dot_general(
        gathered_q, item_embeddings, (((1,), (1,)), ((), ())), preferred_element_type=jnp.float32
    ).reshape(panel, blocks_here, blk)
    local_blocks = base + jnp.arange(blocks_here, dtype=jnp.int32)
    onehot = gathered_ids[:, None, :] == local_blocks[None, :, None]
    valid = jnp.any(onehot, axis=2)[:, :, None]
    teach_local = jnp.einsum(
        "qbs,qsk->qbk",
        onehot.astype(jnp.bfloat16),
        teach_bf.reshape(panel, slots, blk),
        preferred_element_type=jnp.float32,
    )
    target = jnp.exp(teach_local - lse_t[:, None, None])

    masked = jnp.where(valid, scores, -jnp.inf)
    m_part = jnp.max(masked, axis=(1, 2))
    l_part = jnp.sum(jnp.where(valid, jnp.exp(scores - m_part[:, None, None]), 0.0), axis=(1, 2))
    d_part = jnp.sum(jnp.where(valid, target * (teach_local - scores), 0.0), axis=(1, 2))
    parts = lax.all_gather(jnp.stack([m_part, l_part, d_part]), "item", axis=0)
    m_all, l_all, d_all = parts[:, 0], parts[:, 1], parts[:, 2]
    m_s = jnp.max(m_all, axis=0)
    lse_s = m_s + jnp.log(jnp.sum(l_all * jnp.exp(m_all - m_s[None, :]), axis=0))
    row_loss = jnp.sum(jnp.sum(d_all, axis=0) - lse_t + lse_s)

    probs = jnp.exp(scores - lse_s[:, None, None])
    coeff = jnp.where(valid, probs - target, 0.0).astype(jnp.bfloat16)
    dense_rows = coeff.reshape(panel, own_items)

    question_grads = lax.psum_scatter(
        jnp.dot(dense_rows, item_embeddings, preferred_element_type=jnp.float32),
        "item",
        scatter_dimension=0,
        tiled=True,
    )
    item_part = lax.dot_general(
        dense_rows, gathered_q, (((0,), (0,)), ((), ())), preferred_element_type=jnp.float32
    )
    extra = jnp.zeros((8, width), jnp.float32).at[0, 0].set(row_loss)
    reduced = lax.psum(jnp.concatenate([item_part, extra], axis=0), "pb")
    item_grads = reduced[:own_items]
    count_all = panel * lax.axis_size("pb")
    loss = reduced[own_items, 0] / count_all
    return (loss, question_grads, item_grads)


def solution(mesh):
    return jax.shard_map(
        shards,
        mesh=mesh,
        in_specs=(
            P(("pb", "item"), None),
            P("item", None),
            P(("pb", "item"), None),
            P(("pb", "item"), None, None),
        ),
        out_specs=(P(), P(("pb", "item"), None), P("item", None)),
        check_vma=False,
    )
```

```python
import jax
import jax.numpy as jnp
from jax import lax
from jax.sharding import Mesh, PartitionSpec as P


ITEM = ("y", "z", "c")


def row_lse(values):
    top = jnp.max(values, axis=1)
    return top + jnp.log(jnp.sum(jnp.exp(values - top[:, None]), axis=1))


def shards(questions, item_embeddings, block_ids, teacher_scores):
    qdev, width = questions.shape
    slots = block_ids.shape[1]
    blk = teacher_scores.shape[2]
    own_items = item_embeddings.shape[0]
    blocks_here = own_items // blk
    nitem = lax.axis_size(ITEM)
    panel = qdev * nitem
    cand = slots * blk
    base = lax.axis_index(ITEM) * blocks_here

    packed = jnp.concatenate(
        [
            questions,
            teacher_scores.reshape(qdev, cand),
            block_ids.astype(jnp.bfloat16),
        ],
        axis=1,
    )
    gathered = packed
    for axis in ("y", "z", "c"):
        gathered = lax.all_gather(gathered, axis, axis=0, tiled=True)
    ny, nz, nc = lax.axis_size("y"), lax.axis_size("z"), lax.axis_size("c")
    gathered_q = gathered[:, :width]
    teach_bf = gathered[:, width : width + cand]
    gathered_ids = gathered[:, width + cand :].astype(jnp.int32)

    teach_rows = teach_bf.astype(jnp.float32)
    lse_t = row_lse(teach_rows)

    scores = lax.dot_general(
        gathered_q, item_embeddings, (((1,), (1,)), ((), ())), preferred_element_type=jnp.float32
    ).reshape(panel, blocks_here, blk)
    local_blocks = base + jnp.arange(blocks_here, dtype=jnp.int32)
    onehot = gathered_ids[:, None, :] == local_blocks[None, :, None]
    valid = jnp.any(onehot, axis=2)[:, :, None]
    teach_local = jnp.einsum(
        "qbs,qsk->qbk",
        onehot.astype(jnp.bfloat16),
        teach_bf.reshape(panel, slots, blk),
        preferred_element_type=jnp.float32,
    )
    target = jnp.exp(teach_local - lse_t[:, None, None])

    masked = jnp.where(valid, scores, -jnp.inf)
    m_part = jnp.max(masked, axis=(1, 2))
    l_part = jnp.sum(jnp.where(valid, jnp.exp(scores - m_part[:, None, None]), 0.0), axis=(1, 2))
    d_part = jnp.sum(jnp.where(valid, target * (teach_local - scores), 0.0), axis=(1, 2))
    stacked = jnp.stack([m_part, l_part, d_part])
    parts = lax.all_to_all(
        jnp.broadcast_to(stacked[None], (nitem,) + stacked.shape), ITEM, 0, 0, tiled=False
    )
    m_all, l_all, d_all = parts[:, 0], parts[:, 1], parts[:, 2]
    m_s = jnp.max(m_all, axis=0)
    lse_s = m_s + jnp.log(jnp.sum(l_all * jnp.exp(m_all - m_s[None, :]), axis=0))
    row_loss = jnp.sum(jnp.sum(d_all, axis=0) - lse_t + lse_s)

    probs = jnp.exp(scores - lse_s[:, None, None])
    coeff = jnp.where(valid, probs - target, 0.0).astype(jnp.bfloat16)
    dense_rows = coeff.reshape(panel, own_items)

    qg = jnp.dot(dense_rows, item_embeddings, preferred_element_type=jnp.float32)
    qg = qg.reshape(nc, nz, ny, qdev, width).transpose(2, 1, 0, 3, 4).reshape(nitem, qdev, width)
    question_grads = jnp.sum(lax.all_to_all(qg, ITEM, 0, 0, tiled=False), axis=0)
    item_part = lax.dot_general(
        dense_rows, gathered_q, (((0,), (0,)), ((), ())), preferred_element_type=jnp.float32
    )
    extra = jnp.zeros((8, width), jnp.float32).at[0, 0].set(row_loss)
    reduced = lax.psum(jnp.concatenate([item_part, extra], axis=0), "pb")
    item_grads = reduced[:own_items]
    count_all = panel * lax.axis_size("pb")
    loss = reduced[own_items, 0] / count_all
    return (loss, question_grads, item_grads)


def solution(mesh):
    npb, nitem = mesh.devices.shape
    ncore = 2
    nz = 8 if nitem % (8 * ncore) == 0 else 1
    fine = Mesh(mesh.devices.reshape(npb, nitem // (nz * ncore), nz, ncore), ("pb",) + ITEM)
    qspec = ("pb",) + ITEM
    return jax.shard_map(
        shards,
        mesh=fine,
        in_specs=(
            P(qspec, None),
            P(ITEM, None),
            P(qspec, None),
            P(qspec, None, None),
        ),
        out_specs=(P(), P(qspec, None), P(ITEM, None)),
        check_vma=False,
    )
```

```python
import jax
import jax.numpy as jnp
from jax import lax
from jax.sharding import Mesh, PartitionSpec as P


ITEM = ("y", "z", "c")


def row_lse(values):
    top = jnp.max(values, axis=1)
    return top + jnp.log(jnp.sum(jnp.exp(values - top[:, None]), axis=1))


def shards(questions, item_embeddings, block_ids, teacher_scores):
    qdev, width = questions.shape
    slots = block_ids.shape[1]
    blk = teacher_scores.shape[2]
    own_items = item_embeddings.shape[0]
    blocks_here = own_items // blk
    nitem = lax.axis_size(ITEM)
    panel = qdev * nitem
    cand = slots * blk
    base = lax.axis_index(ITEM) * blocks_here

    packed = jnp.concatenate(
        [
            questions,
            teacher_scores.reshape(qdev, cand),
            block_ids.astype(jnp.bfloat16),
        ],
        axis=1,
    )
    gathered = packed
    for axis in ("y", "z", "c"):
        gathered = lax.all_gather(gathered, axis, axis=0, tiled=True)
    ny, nz, nc = lax.axis_size("y"), lax.axis_size("z"), lax.axis_size("c")
    gathered_q = gathered[:, :width]
    teach_bf = gathered[:, width : width + cand]
    gathered_ids = gathered[:, width + cand :].astype(jnp.int32)

    all_q = lax.all_gather(gathered_q, "pb", axis=0, tiled=True)
    npb = lax.axis_size("pb")

    teach_rows = teach_bf.astype(jnp.float32)
    lse_t = row_lse(teach_rows)

    scores = lax.dot_general(
        gathered_q, item_embeddings, (((1,), (1,)), ((), ())), preferred_element_type=jnp.float32
    ).reshape(panel, blocks_here, blk)
    local_blocks = base + jnp.arange(blocks_here, dtype=jnp.int32)
    onehot = gathered_ids[:, None, :] == local_blocks[None, :, None]
    valid = jnp.any(onehot, axis=2)[:, :, None]
    teach_local = jnp.einsum(
        "qbs,qsk->qbk",
        onehot.astype(jnp.bfloat16),
        teach_bf.reshape(panel, slots, blk),
        preferred_element_type=jnp.float32,
    )
    target = jnp.exp(teach_local - lse_t[:, None, None])

    masked = jnp.where(valid, scores, -jnp.inf)
    m_part = jnp.max(masked, axis=(1, 2))
    l_part = jnp.sum(jnp.where(valid, jnp.exp(scores - m_part[:, None, None]), 0.0), axis=(1, 2))
    d_part = jnp.sum(jnp.where(valid, target * (teach_local - scores), 0.0), axis=(1, 2))
    stacked = jnp.stack([m_part, l_part, d_part])
    parts = lax.all_to_all(
        jnp.broadcast_to(stacked[None], (nitem,) + stacked.shape), ITEM, 0, 0, tiled=False
    )
    m_all, l_all, d_all = parts[:, 0], parts[:, 1], parts[:, 2]
    m_s = jnp.max(m_all, axis=0)
    lse_s = m_s + jnp.log(jnp.sum(l_all * jnp.exp(m_all - m_s[None, :]), axis=0))
    row_loss = jnp.sum(jnp.sum(d_all, axis=0) - lse_t + lse_s)

    probs = jnp.exp(scores - lse_s[:, None, None])
    coeff = jnp.where(valid, probs - target, 0.0).astype(jnp.bfloat16)
    dense_rows = coeff.reshape(panel, own_items)

    qg = jnp.dot(dense_rows, item_embeddings, preferred_element_type=jnp.float32)
    qg = qg.reshape(nc, nz, ny, qdev, width).transpose(2, 1, 0, 3, 4).reshape(nitem, qdev, width)
    question_grads = jnp.sum(lax.all_to_all(qg, ITEM, 0, 0, tiled=False), axis=0)
    hi = lax.reduce_precision(row_loss, exponent_bits=8, mantissa_bits=7)
    rest = row_loss - hi
    mid = lax.reduce_precision(rest, exponent_bits=8, mantissa_bits=7)
    lo = lax.reduce_precision(rest - mid, exponent_bits=8, mantissa_bits=7)
    pieces = jnp.zeros((8, own_items), jnp.float32).at[0, :3].set(jnp.stack([hi, mid, lo]))
    payload = jnp.concatenate([dense_rows, pieces.astype(jnp.bfloat16)], axis=0)
    got = lax.all_to_all(
        jnp.broadcast_to(payload[None], (npb,) + payload.shape), "pb", 0, 0, tiled=False
    )
    coeff_all = got[:, :panel].reshape(npb * panel, own_items)
    item_grads = lax.dot_general(
        coeff_all, all_q, (((0,), (0,)), ((), ())), preferred_element_type=jnp.float32
    )
    loss_pieces = got[:, panel, :3].astype(jnp.float32)
    total = jnp.sum(loss_pieces[:, 0] + loss_pieces[:, 1] + loss_pieces[:, 2])
    loss = total / (panel * npb)
    return (loss, question_grads, item_grads)


def solution(mesh):
    npb, nitem = mesh.devices.shape
    ncore = 2
    nz = 8 if nitem % (8 * ncore) == 0 else 1
    fine = Mesh(mesh.devices.reshape(npb, nitem // (nz * ncore), nz, ncore), ("pb",) + ITEM)
    qspec = ("pb",) + ITEM
    return jax.shard_map(
        shards,
        mesh=fine,
        in_specs=(
            P(qspec, None),
            P(ITEM, None),
            P(qspec, None),
            P(qspec, None, None),
        ),
        out_specs=(P(), P(qspec, None), P(ITEM, None)),
        check_vma=False,
    )
```

```python
import jax
import jax.numpy as jnp
from jax import lax
from jax.sharding import Mesh, PartitionSpec as P


ITEM = ("y", "z", "c")


def row_lse(values):
    top = jnp.max(values, axis=1)
    return top + jnp.log(jnp.sum(jnp.exp(values - top[:, None]), axis=1))


def bf16_pieces(x):
    hi = lax.reduce_precision(x, exponent_bits=8, mantissa_bits=7)
    rest = x - hi
    mid = lax.reduce_precision(rest, exponent_bits=8, mantissa_bits=7)
    lo = lax.reduce_precision(rest - mid, exponent_bits=8, mantissa_bits=7)
    return jnp.stack([hi, mid, lo], axis=-1)


def shards(questions, item_embeddings, block_ids, teacher_scores):
    qdev, width = questions.shape
    slots = block_ids.shape[1]
    blk = teacher_scores.shape[2]
    own_items = item_embeddings.shape[0]
    blocks_here = own_items // blk
    nitem = lax.axis_size(ITEM)
    nblk = nitem * blocks_here
    panel = qdev * nitem
    base = lax.axis_index(ITEM) * blocks_here

    named = block_ids[:, :, None] == jnp.arange(nblk, dtype=jnp.int32)[None, None, :]
    routed = jnp.einsum(
        "qjb,qjk->bqk",
        named.astype(jnp.bfloat16),
        teacher_scores,
        preferred_element_type=jnp.float32,
    ).astype(jnp.bfloat16)
    routed = routed.reshape(nitem, blocks_here, qdev, blk).transpose(0, 2, 1, 3)
    teach_local = lax.all_to_all(routed, ITEM, 0, 0, tiled=False)
    teach_local = teach_local.reshape(panel, blocks_here, blk).astype(jnp.float32)

    mask = jnp.any(named, axis=1).astype(jnp.bfloat16)
    lse_own = bf16_pieces(row_lse(teacher_scores.astype(jnp.float32).reshape(qdev, slots * blk)))
    tail = jnp.zeros((qdev, 128), jnp.bfloat16).at[:, :3].set(lse_own.astype(jnp.bfloat16))
    packed = jnp.concatenate([questions, mask, tail], axis=1)
    gathered = packed
    for axis in ("c", "z", "y"):
        gathered = lax.all_gather(gathered, axis, axis=0, tiled=True)
    gathered_q = gathered[:, :width]
    valid = lax.dynamic_slice_in_dim(gathered, width + base, blocks_here, axis=1) > 0.5
    valid = valid[:, :, None]
    lse_parts = gathered[:, width + nblk : width + nblk + 3].astype(jnp.float32)
    lse_t = lse_parts[:, 0] + lse_parts[:, 1] + lse_parts[:, 2]

    scores = lax.dot_general(
        gathered_q, item_embeddings, (((1,), (1,)), ((), ())), preferred_element_type=jnp.float32
    ).reshape(panel, blocks_here, blk)
    target = jnp.exp(teach_local - lse_t[:, None, None])

    masked = jnp.where(valid, scores, -jnp.inf)
    m_part = jnp.max(masked, axis=(1, 2))
    l_part = jnp.sum(jnp.where(valid, jnp.exp(scores - m_part[:, None, None]), 0.0), axis=(1, 2))
    d_part = jnp.sum(jnp.where(valid, target * (teach_local - scores), 0.0), axis=(1, 2))
    stacked = jnp.stack([m_part, l_part, d_part])
    parts = lax.all_to_all(
        jnp.broadcast_to(stacked[None], (nitem,) + stacked.shape), ITEM, 0, 0, tiled=False
    )
    m_all, l_all, d_all = parts[:, 0], parts[:, 1], parts[:, 2]
    m_s = jnp.max(m_all, axis=0)
    lse_s = m_s + jnp.log(jnp.sum(l_all * jnp.exp(m_all - m_s[None, :]), axis=0))
    row_loss = jnp.sum(jnp.sum(d_all, axis=0) - lse_t + lse_s)

    probs = jnp.exp(scores - lse_s[:, None, None])
    coeff = jnp.where(valid, probs - target, 0.0).astype(jnp.bfloat16)
    dense_rows = coeff.reshape(panel, own_items)

    qg = jnp.dot(dense_rows, item_embeddings, preferred_element_type=jnp.float32)
    qg = qg.reshape(nitem, qdev, width)
    question_grads = jnp.sum(lax.all_to_all(qg, ITEM, 0, 0, tiled=False), axis=0)
    item_part = lax.dot_general(
        dense_rows, gathered_q, (((0,), (0,)), ((), ())), preferred_element_type=jnp.float32
    )
    extra = jnp.zeros((8, width), jnp.float32).at[0, 0].set(row_loss)
    reduced = lax.psum(jnp.concatenate([item_part, extra], axis=0), "pb")
    item_grads = reduced[:own_items]
    count_all = panel * lax.axis_size("pb")
    loss = reduced[own_items, 0] / count_all
    return (loss, question_grads, item_grads)


def solution(mesh):
    npb, nitem = mesh.devices.shape
    ncore = 2
    nz = 8 if nitem % (8 * ncore) == 0 else 1
    fine = Mesh(mesh.devices.reshape(npb, nitem // (nz * ncore), nz, ncore), ("pb",) + ITEM)
    qspec = ("pb",) + ITEM
    return jax.shard_map(
        shards,
        mesh=fine,
        in_specs=(
            P(qspec, None),
            P(ITEM, None),
            P(qspec, None),
            P(qspec, None, None),
        ),
        out_specs=(P(), P(qspec, None), P(ITEM, None)),
        check_vma=False,
    )
```

```python
import jax
import jax.numpy as jnp
from jax import lax
from jax.sharding import Mesh, PartitionSpec as P


ITEM = ("y", "z", "c")


def row_lse(values):
    top = jnp.max(values, axis=1)
    return top + jnp.log(jnp.sum(jnp.exp(values - top[:, None]), axis=1))


def bf16_pieces(x):
    hi = lax.reduce_precision(x, exponent_bits=8, mantissa_bits=7)
    rest = x - hi
    mid = lax.reduce_precision(rest, exponent_bits=8, mantissa_bits=7)
    lo = lax.reduce_precision(rest - mid, exponent_bits=8, mantissa_bits=7)
    return jnp.stack([hi, mid, lo], axis=-1)


def shards(questions, item_embeddings, block_ids, teacher_scores):
    qdev, width = questions.shape
    slots = block_ids.shape[1]
    blk = teacher_scores.shape[2]
    own_items = item_embeddings.shape[0]
    blocks_here = own_items // blk
    nitem = lax.axis_size(ITEM)
    nblk = nitem * blocks_here
    panel = qdev * nitem
    base = lax.axis_index(ITEM) * blocks_here

    named = block_ids[:, :, None] == jnp.arange(nblk, dtype=jnp.int32)[None, None, :]
    routed = jnp.einsum(
        "qjb,qjk->bqk",
        named.astype(jnp.bfloat16),
        teacher_scores,
        preferred_element_type=jnp.float32,
    ).astype(jnp.bfloat16)
    routed = routed.reshape(nitem, blocks_here, qdev, blk).transpose(0, 2, 1, 3)
    teach_local = lax.all_to_all(routed, ITEM, 0, 0, tiled=False)
    teach_local = teach_local.reshape(panel, blocks_here, blk).astype(jnp.float32)

    mask = jnp.any(named, axis=1).astype(jnp.bfloat16)
    lse_own = bf16_pieces(row_lse(teacher_scores.astype(jnp.float32).reshape(qdev, slots * blk)))
    tail = jnp.zeros((qdev, 128), jnp.bfloat16).at[:, :3].set(lse_own.astype(jnp.bfloat16))
    packed = jnp.concatenate([questions, mask, tail], axis=1)
    gathered = packed
    for axis in ("c", "z", "y"):
        gathered = lax.all_gather(gathered, axis, axis=0, tiled=True)
    gathered_q = gathered[:, :width]
    valid = lax.dynamic_slice_in_dim(gathered, width + base, blocks_here, axis=1) > 0.5
    valid = valid[:, :, None]
    all_q = lax.all_gather(gathered_q, "pb", axis=0)
    lse_parts = gathered[:, width + nblk : width + nblk + 3].astype(jnp.float32)
    lse_t = lse_parts[:, 0] + lse_parts[:, 1] + lse_parts[:, 2]

    scores = lax.dot_general(
        gathered_q, item_embeddings, (((1,), (1,)), ((), ())), preferred_element_type=jnp.float32
    ).reshape(panel, blocks_here, blk)
    target = jnp.exp(teach_local - lse_t[:, None, None])

    masked = jnp.where(valid, scores, -jnp.inf)
    m_part = jnp.max(masked, axis=(1, 2))
    l_part = jnp.sum(jnp.where(valid, jnp.exp(scores - m_part[:, None, None]), 0.0), axis=(1, 2))
    d_part = jnp.sum(jnp.where(valid, target * (teach_local - scores), 0.0), axis=(1, 2))
    stacked = jnp.stack([m_part, l_part, d_part])
    parts = lax.all_to_all(
        jnp.broadcast_to(stacked[None], (nitem,) + stacked.shape), ITEM, 0, 0, tiled=False
    )
    m_all, l_all, d_all = parts[:, 0], parts[:, 1], parts[:, 2]
    m_s = jnp.max(m_all, axis=0)
    lse_s = m_s + jnp.log(jnp.sum(l_all * jnp.exp(m_all - m_s[None, :]), axis=0))
    row_loss = jnp.sum(jnp.sum(d_all, axis=0) - lse_t + lse_s)

    probs = jnp.exp(scores - lse_s[:, None, None])
    coeff = jnp.where(valid, probs - target, 0.0).astype(jnp.bfloat16)
    dense_rows = coeff.reshape(panel, own_items)

    qg = jnp.dot(dense_rows, item_embeddings, preferred_element_type=jnp.float32)
    qg = qg.reshape(nitem, qdev, width)
    question_grads = jnp.sum(lax.all_to_all(qg, ITEM, 0, 0, tiled=False), axis=0)
    npb = lax.axis_size("pb")
    pieces = jnp.zeros((8, own_items), jnp.float32).at[0, :3].set(bf16_pieces(row_loss))
    payload = jnp.concatenate([dense_rows, pieces.astype(jnp.bfloat16)], axis=0)
    payload, all_q = lax.optimization_barrier((payload, all_q))
    got = lax.all_gather(payload, "pb", axis=0)
    item_grads = lax.dot_general(
        got[:, :panel], all_q, (((0, 1), (0, 1)), ((), ())), preferred_element_type=jnp.float32
    )
    loss_parts = got[:, panel, :3].astype(jnp.float32)
    total = jnp.sum(loss_parts[:, 0] + loss_parts[:, 1] + loss_parts[:, 2])
    loss = total / (panel * npb)
    return (loss, question_grads, item_grads)


def solution(mesh):
    npb, nitem = mesh.devices.shape
    ncore = 2
    nz = 8 if nitem % (8 * ncore) == 0 else 1
    fine = Mesh(mesh.devices.reshape(npb, nitem // (nz * ncore), nz, ncore), ("pb",) + ITEM)
    qspec = ("pb",) + ITEM
    return jax.shard_map(
        shards,
        mesh=fine,
        in_specs=(
            P(qspec, None),
            P(ITEM, None),
            P(qspec, None),
            P(qspec, None, None),
        ),
        out_specs=(P(), P(qspec, None), P(ITEM, None)),
        check_vma=False,
    )
```

```python
import jax
import jax.numpy as jnp
from jax import lax
from jax.sharding import Mesh, PartitionSpec as P


ITEM = ("y", "z", "c")


def row_lse(values):
    top = jnp.max(values, axis=1)
    return top + jnp.log(jnp.sum(jnp.exp(values - top[:, None]), axis=1))


def bf16_pieces(x):
    hi = lax.reduce_precision(x, exponent_bits=8, mantissa_bits=7)
    rest = x - hi
    mid = lax.reduce_precision(rest, exponent_bits=8, mantissa_bits=7)
    lo = lax.reduce_precision(rest - mid, exponent_bits=8, mantissa_bits=7)
    return jnp.stack([hi, mid, lo], axis=-1)


def shards(questions, item_embeddings, block_ids, teacher_scores):
    qdev, width = questions.shape
    slots = block_ids.shape[1]
    blk = teacher_scores.shape[2]
    own_items = item_embeddings.shape[0]
    blocks_here = own_items // blk
    nitem = lax.axis_size(ITEM)
    nblk = nitem * blocks_here
    panel = qdev * nitem
    base = lax.axis_index(ITEM) * blocks_here

    named = block_ids[:, :, None] == jnp.arange(nblk, dtype=jnp.int32)[None, None, :]
    routed = jnp.einsum(
        "qjb,qjk->bqk",
        named.astype(jnp.bfloat16),
        teacher_scores,
        preferred_element_type=jnp.float32,
    ).astype(jnp.bfloat16)
    routed = routed.reshape(nitem, blocks_here, qdev, blk).transpose(0, 2, 1, 3)
    routed = routed.reshape(nitem, qdev, own_items)

    mask = jnp.any(named, axis=1).astype(jnp.bfloat16)
    lse_own = bf16_pieces(row_lse(teacher_scores.astype(jnp.float32).reshape(qdev, slots * blk)))
    tail = jnp.zeros((qdev, 128), jnp.bfloat16).at[:, :3].set(lse_own.astype(jnp.bfloat16))
    packed = jnp.concatenate([questions, mask, tail], axis=1)
    send = jnp.concatenate(
        [jnp.broadcast_to(packed[None], (nitem,) + packed.shape), routed], axis=2
    )
    recv = lax.all_to_all(send, ITEM, 0, 0, tiled=False).reshape(panel, -1)
    ncols = packed.shape[1]
    gathered = recv[:, :ncols]
    teach_local = recv[:, ncols:].reshape(panel, blocks_here, blk).astype(jnp.float32)
    gathered_q = gathered[:, :width]
    valid = lax.dynamic_slice_in_dim(gathered, width + base, blocks_here, axis=1) > 0.5
    valid = valid[:, :, None]
    lse_parts = gathered[:, width + nblk : width + nblk + 3].astype(jnp.float32)
    lse_t = lse_parts[:, 0] + lse_parts[:, 1] + lse_parts[:, 2]

    scores = lax.dot_general(
        gathered_q, item_embeddings, (((1,), (1,)), ((), ())), preferred_element_type=jnp.float32
    ).reshape(panel, blocks_here, blk)
    target = jnp.exp(teach_local - lse_t[:, None, None])

    masked = jnp.where(valid, scores, -jnp.inf)
    m_part = jnp.max(masked, axis=(1, 2))
    l_part = jnp.sum(jnp.where(valid, jnp.exp(scores - m_part[:, None, None]), 0.0), axis=(1, 2))
    d_part = jnp.sum(jnp.where(valid, target * (teach_local - scores), 0.0), axis=(1, 2))
    stacked = jnp.stack([m_part, l_part, d_part])
    parts = lax.all_to_all(
        jnp.broadcast_to(stacked[None], (nitem,) + stacked.shape), ITEM, 0, 0, tiled=False
    )
    m_all, l_all, d_all = parts[:, 0], parts[:, 1], parts[:, 2]
    m_s = jnp.max(m_all, axis=0)
    lse_s = m_s + jnp.log(jnp.sum(l_all * jnp.exp(m_all - m_s[None, :]), axis=0))
    row_loss = jnp.sum(jnp.sum(d_all, axis=0) - lse_t + lse_s)

    probs = jnp.exp(scores - lse_s[:, None, None])
    coeff = jnp.where(valid, probs - target, 0.0).astype(jnp.bfloat16)
    dense_rows = coeff.reshape(panel, own_items)

    qg = jnp.dot(dense_rows, item_embeddings, preferred_element_type=jnp.float32)
    qg = qg.reshape(nitem, qdev, width)
    question_grads = jnp.sum(lax.all_to_all(qg, ITEM, 0, 0, tiled=False), axis=0)
    item_part = lax.dot_general(
        dense_rows, gathered_q, (((0,), (0,)), ((), ())), preferred_element_type=jnp.float32
    )
    extra = jnp.zeros((8, width), jnp.float32).at[0, 0].set(row_loss)
    reduced = lax.psum(jnp.concatenate([item_part, extra], axis=0), "pb")
    item_grads = reduced[:own_items]
    count_all = panel * lax.axis_size("pb")
    loss = reduced[own_items, 0] / count_all
    return (loss, question_grads, item_grads)


def solution(mesh):
    npb, nitem = mesh.devices.shape
    ncore = 2
    nz = 8 if nitem % (8 * ncore) == 0 else 1
    fine = Mesh(mesh.devices.reshape(npb, nitem // (nz * ncore), nz, ncore), ("pb",) + ITEM)
    qspec = ("pb",) + ITEM
    return jax.shard_map(
        shards,
        mesh=fine,
        in_specs=(
            P(qspec, None),
            P(ITEM, None),
            P(qspec, None),
            P(qspec, None, None),
        ),
        out_specs=(P(), P(qspec, None), P(ITEM, None)),
        check_vma=False,
    )
```

```python
import jax
import jax.numpy as jnp
from jax import lax
from jax.sharding import Mesh, PartitionSpec as P


ITEM = ("y", "z", "c")


def row_lse(values):
    top = jnp.max(values, axis=1)
    return top + jnp.log(jnp.sum(jnp.exp(values - top[:, None]), axis=1))


def bf16_pieces(x):
    hi = lax.reduce_precision(x, exponent_bits=8, mantissa_bits=7)
    rest = x - hi
    mid = lax.reduce_precision(rest, exponent_bits=8, mantissa_bits=7)
    lo = lax.reduce_precision(rest - mid, exponent_bits=8, mantissa_bits=7)
    return jnp.stack([hi, mid, lo], axis=-1)


def shards(questions, item_embeddings, block_ids, teacher_scores):
    qdev, width = questions.shape
    slots = block_ids.shape[1]
    blk = teacher_scores.shape[2]
    own_items = item_embeddings.shape[0]
    blocks_here = own_items // blk
    nitem = lax.axis_size(ITEM)
    nblk = nitem * blocks_here
    panel = qdev * nitem
    base = lax.axis_index(ITEM) * blocks_here

    named = block_ids[:, :, None] == jnp.arange(nblk, dtype=jnp.int32)[None, None, :]
    routed = jnp.einsum(
        "qjb,qjk->bqk",
        named.astype(jnp.bfloat16),
        teacher_scores,
        preferred_element_type=jnp.float32,
    ).astype(jnp.bfloat16)
    routed = routed.reshape(nitem, blocks_here, qdev, blk).transpose(0, 2, 1, 3)
    routed = routed.reshape(nitem, qdev, own_items)

    mask = jnp.any(named, axis=1).astype(jnp.bfloat16).reshape(qdev, nitem, blocks_here)
    lse_own = bf16_pieces(row_lse(teacher_scores.astype(jnp.float32).reshape(qdev, slots * blk)))
    tail = jnp.zeros((nitem, qdev, 128), jnp.bfloat16)
    tail = tail.at[:, :, :blocks_here].set(mask.transpose(1, 0, 2))
    tail = tail.at[:, :, blocks_here : blocks_here + 3].set(
        jnp.broadcast_to(lse_own.astype(jnp.bfloat16)[None], (nitem, qdev, 3))
    )
    send = jnp.concatenate(
        [jnp.broadcast_to(questions[None], (nitem, qdev, width)), routed, tail], axis=2
    )
    recv = lax.all_to_all(send, ITEM, 0, 0, tiled=False).reshape(panel, -1)
    gathered_q = recv[:, :width]
    teach_local = recv[:, width : width + own_items]
    teach_local = teach_local.reshape(panel, blocks_here, blk).astype(jnp.float32)
    valid = recv[:, width + own_items : width + own_items + blocks_here] > 0.5
    valid = valid[:, :, None]
    lse_parts = recv[:, width + own_items + blocks_here : width + own_items + blocks_here + 3]
    lse_parts = lse_parts.astype(jnp.float32)
    lse_t = lse_parts[:, 0] + lse_parts[:, 1] + lse_parts[:, 2]
    all_q = lax.all_gather(gathered_q, "pb", axis=0)

    scores = lax.dot_general(
        gathered_q, item_embeddings, (((1,), (1,)), ((), ())), preferred_element_type=jnp.float32
    ).reshape(panel, blocks_here, blk)
    target = jnp.exp(teach_local - lse_t[:, None, None])

    masked = jnp.where(valid, scores, -jnp.inf)
    m_part = jnp.max(masked, axis=(1, 2))
    l_part = jnp.sum(jnp.where(valid, jnp.exp(scores - m_part[:, None, None]), 0.0), axis=(1, 2))
    d_part = jnp.sum(jnp.where(valid, target * (teach_local - scores), 0.0), axis=(1, 2))
    stacked = jnp.stack([m_part, l_part, d_part])
    parts = lax.all_to_all(
        jnp.broadcast_to(stacked[None], (nitem,) + stacked.shape), ITEM, 0, 0, tiled=False
    )
    m_all, l_all, d_all = parts[:, 0], parts[:, 1], parts[:, 2]
    m_s = jnp.max(m_all, axis=0)
    lse_s = m_s + jnp.log(jnp.sum(l_all * jnp.exp(m_all - m_s[None, :]), axis=0))
    row_loss = jnp.sum(jnp.sum(d_all, axis=0) - lse_t + lse_s)

    probs = jnp.exp(scores - lse_s[:, None, None])
    coeff = jnp.where(valid, probs - target, 0.0).astype(jnp.bfloat16)
    dense_rows = coeff.reshape(panel, own_items)

    qg = jnp.dot(dense_rows, item_embeddings, preferred_element_type=jnp.float32)
    qg = qg.reshape(nitem, qdev, width)
    question_grads = jnp.sum(lax.all_to_all(qg, ITEM, 0, 0, tiled=False), axis=0)
    npb = lax.axis_size("pb")
    pieces = jnp.zeros((8, own_items), jnp.float32).at[0, :3].set(bf16_pieces(row_loss))
    payload = jnp.concatenate([dense_rows, pieces.astype(jnp.bfloat16)], axis=0)
    payload, all_q = lax.optimization_barrier((payload, all_q))
    got = lax.all_gather(payload, "pb", axis=0)
    item_grads = lax.dot_general(
        got[:, :panel], all_q, (((0, 1), (0, 1)), ((), ())), preferred_element_type=jnp.float32
    )
    loss_parts = got[:, panel, :3].astype(jnp.float32)
    total = jnp.sum(loss_parts[:, 0] + loss_parts[:, 1] + loss_parts[:, 2])
    loss = total / (panel * npb)
    return (loss, question_grads, item_grads)


def solution(mesh):
    npb, nitem = mesh.devices.shape
    ncore = 2
    nz = 8 if nitem % (8 * ncore) == 0 else 1
    fine = Mesh(mesh.devices.reshape(npb, nitem // (nz * ncore), nz, ncore), ("pb",) + ITEM)
    qspec = ("pb",) + ITEM
    return jax.shard_map(
        shards,
        mesh=fine,
        in_specs=(
            P(qspec, None),
            P(ITEM, None),
            P(qspec, None),
            P(qspec, None, None),
        ),
        out_specs=(P(), P(qspec, None), P(ITEM, None)),
        check_vma=False,
    )
```

```python
import jax
import jax.numpy as jnp
from jax import lax
from jax.sharding import Mesh, PartitionSpec as P


ITEM = ("y", "z", "c")


def row_lse(values):
    top = jnp.max(values, axis=1)
    return top + jnp.log(jnp.sum(jnp.exp(values - top[:, None]), axis=1))


def bf16_pieces(x):
    hi = lax.reduce_precision(x, exponent_bits=8, mantissa_bits=7)
    rest = x - hi
    mid = lax.reduce_precision(rest, exponent_bits=8, mantissa_bits=7)
    lo = lax.reduce_precision(rest - mid, exponent_bits=8, mantissa_bits=7)
    return jnp.stack([hi, mid, lo], axis=-1)


def shards(questions, item_embeddings, block_ids, teacher_scores):
    qdev, width = questions.shape
    slots = block_ids.shape[1]
    blk = teacher_scores.shape[2]
    own_items = item_embeddings.shape[0]
    blocks_here = own_items // blk
    nitem = lax.axis_size(ITEM)
    nblk = nitem * blocks_here
    panel = qdev * nitem
    base = lax.axis_index(ITEM) * blocks_here

    named = block_ids[:, :, None] == jnp.arange(nblk, dtype=jnp.int32)[None, None, :]
    routed = jnp.einsum(
        "qjb,qjk->bqk",
        named.astype(jnp.bfloat16),
        teacher_scores,
        preferred_element_type=jnp.float32,
    ).astype(jnp.bfloat16)
    routed = routed.reshape(nitem, blocks_here, qdev, blk).transpose(0, 2, 1, 3)
    routed = routed.reshape(nitem, qdev, own_items)

    mask = jnp.any(named, axis=1).astype(jnp.bfloat16).reshape(qdev, nitem, blocks_here)
    lse_own = bf16_pieces(row_lse(teacher_scores.astype(jnp.float32).reshape(qdev, slots * blk)))
    tail = jnp.zeros((nitem, qdev, 128), jnp.bfloat16)
    tail = tail.at[:, :, :blocks_here].set(mask.transpose(1, 0, 2))
    tail = tail.at[:, :, blocks_here : blocks_here + 3].set(
        jnp.broadcast_to(lse_own.astype(jnp.bfloat16)[None], (nitem, qdev, 3))
    )
    send = jnp.concatenate(
        [jnp.broadcast_to(questions[None], (nitem, qdev, width)), routed, tail], axis=2
    )
    recv = lax.all_to_all(send, ITEM, 0, 0, tiled=False).reshape(panel, -1)
    gathered_q = recv[:, :width]
    teach_local = recv[:, width : width + own_items]
    teach_local = teach_local.reshape(panel, blocks_here, blk).astype(jnp.float32)
    valid = recv[:, width + own_items : width + own_items + blocks_here] > 0.5
    valid = valid[:, :, None]
    lse_parts = recv[:, width + own_items + blocks_here : width + own_items + blocks_here + 3]
    lse_parts = lse_parts.astype(jnp.float32)
    lse_t = lse_parts[:, 0] + lse_parts[:, 1] + lse_parts[:, 2]
    all_q = lax.all_gather(gathered_q, "pb", axis=0)

    scores = lax.dot_general(
        gathered_q, item_embeddings, (((1,), (1,)), ((), ())), preferred_element_type=jnp.float32
    ).reshape(panel, blocks_here, blk)
    target = jnp.exp(teach_local - lse_t[:, None, None])

    masked = jnp.where(valid, scores, -jnp.inf)
    m_part = jnp.max(masked, axis=(1, 2))
    l_part = jnp.sum(jnp.where(valid, jnp.exp(scores - m_part[:, None, None]), 0.0), axis=(1, 2))
    d_part = jnp.sum(jnp.where(valid, target * (teach_local - scores), 0.0), axis=(1, 2))
    stacked = jnp.stack([m_part, l_part, d_part])
    parts = lax.all_to_all(
        jnp.broadcast_to(stacked[None], (nitem,) + stacked.shape), ITEM, 0, 0, tiled=False
    )
    m_all, l_all, d_all = parts[:, 0], parts[:, 1], parts[:, 2]
    m_s = jnp.max(m_all, axis=0)
    lse_s = m_s + jnp.log(jnp.sum(l_all * jnp.exp(m_all - m_s[None, :]), axis=0))
    row_loss = jnp.sum(jnp.sum(d_all, axis=0) - lse_t + lse_s)

    probs = jnp.exp(scores - lse_s[:, None, None])
    coeff = jnp.where(valid, probs - target, 0.0).astype(jnp.bfloat16)
    dense_rows = coeff.reshape(panel, own_items)

    qg = jnp.dot(dense_rows, item_embeddings, preferred_element_type=jnp.float32)
    ncore = lax.axis_size("c")
    qg = qg.reshape(nitem // ncore, ncore, qdev, width).transpose(1, 0, 2, 3)
    qg = jnp.sum(lax.all_to_all(qg, "c", 0, 0, tiled=False), axis=0)
    question_grads = jnp.sum(lax.all_to_all(qg, ("y", "z"), 0, 0, tiled=False), axis=0)
    npb = lax.axis_size("pb")
    pieces = jnp.zeros((8, own_items), jnp.float32).at[0, :3].set(bf16_pieces(row_loss))
    payload = jnp.concatenate([dense_rows, pieces.astype(jnp.bfloat16)], axis=0)
    payload, all_q = lax.optimization_barrier((payload, all_q))
    got = lax.all_gather(payload, "pb", axis=0)
    item_grads = lax.dot_general(
        got[:, :panel], all_q, (((0, 1), (0, 1)), ((), ())), preferred_element_type=jnp.float32
    )
    loss_parts = got[:, panel, :3].astype(jnp.float32)
    total = jnp.sum(loss_parts[:, 0] + loss_parts[:, 1] + loss_parts[:, 2])
    loss = total / (panel * npb)
    return (loss, question_grads, item_grads)


def solution(mesh):
    npb, nitem = mesh.devices.shape
    ncore = 2
    nz = 8 if nitem % (8 * ncore) == 0 else 1
    fine = Mesh(mesh.devices.reshape(npb, nitem // (nz * ncore), nz, ncore), ("pb",) + ITEM)
    qspec = ("pb",) + ITEM
    return jax.shard_map(
        shards,
        mesh=fine,
        in_specs=(
            P(qspec, None),
            P(ITEM, None),
            P(qspec, None),
            P(qspec, None, None),
        ),
        out_specs=(P(), P(qspec, None), P(ITEM, None)),
        check_vma=False,
    )
```

```python
import jax
import jax.numpy as jnp
from jax import lax
from jax.sharding import Mesh, PartitionSpec as P


ITEM = ("y", "z", "c")


def row_lse(values):
    top = jnp.max(values, axis=1)
    return top + jnp.log(jnp.sum(jnp.exp(values - top[:, None]), axis=1))


def bf16_pieces(x):
    hi = lax.reduce_precision(x, exponent_bits=8, mantissa_bits=7)
    rest = x - hi
    mid = lax.reduce_precision(rest, exponent_bits=8, mantissa_bits=7)
    lo = lax.reduce_precision(rest - mid, exponent_bits=8, mantissa_bits=7)
    return jnp.stack([hi, mid, lo], axis=-1)


def shards(questions, item_embeddings, block_ids, teacher_scores):
    qdev, width = questions.shape
    slots = block_ids.shape[1]
    blk = teacher_scores.shape[2]
    own_items = item_embeddings.shape[0]
    blocks_here = own_items // blk
    nitem = lax.axis_size(ITEM)
    nblk = nitem * blocks_here
    panel = qdev * nitem
    base = lax.axis_index(ITEM) * blocks_here

    named = block_ids[:, :, None] == jnp.arange(nblk, dtype=jnp.int32)[None, None, :]
    routed = jnp.einsum(
        "qjb,qjk->bqk",
        named.astype(jnp.bfloat16),
        teacher_scores,
        preferred_element_type=jnp.float32,
    ).astype(jnp.bfloat16)
    routed = routed.reshape(nitem, blocks_here, qdev, blk).transpose(0, 2, 1, 3)
    routed = routed.reshape(nitem, qdev, own_items)

    ncore = lax.axis_size("c")
    nchip = nitem // ncore
    mask = jnp.any(named, axis=1).astype(jnp.bfloat16).reshape(qdev, nchip, ncore * blocks_here)
    lse_own = bf16_pieces(row_lse(teacher_scores.astype(jnp.float32).reshape(qdev, slots * blk)))
    lse_own = lse_own.astype(jnp.bfloat16)
    nmask = ncore * blocks_here
    tail = jnp.zeros((nchip, qdev, -(-(nmask + 3) // 128) * 128), jnp.bfloat16)
    tail = tail.at[:, :, :nmask].set(mask.transpose(1, 0, 2))
    tail = tail.at[:, :, nmask : nmask + 3].set(jnp.broadcast_to(lse_own[None], (nchip, qdev, 3)))
    routed = routed.reshape(nchip, ncore, qdev, own_items).transpose(0, 2, 1, 3)
    routed = routed.reshape(nchip, qdev, ncore * own_items)
    send = jnp.concatenate(
        [jnp.broadcast_to(questions[None], (nchip, qdev, width)), routed, tail], axis=2
    )
    recv = lax.all_to_all(send, ("y", "z"), 0, 0, tiled=False)
    per_core = []
    for core in range(ncore):
        t0 = width + core * own_items
        m0 = width + ncore * own_items + core * blocks_here
        l0 = width + ncore * own_items + nmask
        tail2 = jnp.zeros((nchip, qdev, -(-(blocks_here + 3) // 128) * 128), jnp.bfloat16)
        tail2 = tail2.at[:, :, :blocks_here].set(recv[:, :, m0 : m0 + blocks_here])
        tail2 = tail2.at[:, :, blocks_here : blocks_here + 3].set(recv[:, :, l0 : l0 + 3])
        per_core.append(
            jnp.concatenate([recv[:, :, :width], recv[:, :, t0 : t0 + own_items], tail2], axis=2)
        )
    recv = lax.all_to_all(jnp.stack(per_core), "c", 0, 0, tiled=False)
    recv = recv.transpose(1, 0, 2, 3).reshape(panel, -1)
    gathered_q = recv[:, :width]
    teach_local = recv[:, width : width + own_items]
    teach_local = teach_local.reshape(panel, blocks_here, blk).astype(jnp.float32)
    valid = recv[:, width + own_items : width + own_items + blocks_here] > 0.5
    valid = valid[:, :, None]
    lse_parts = recv[:, width + own_items + blocks_here : width + own_items + blocks_here + 3]
    lse_parts = lse_parts.astype(jnp.float32)
    lse_t = lse_parts[:, 0] + lse_parts[:, 1] + lse_parts[:, 2]
    all_q = lax.all_gather(gathered_q, "pb", axis=0)

    scores = lax.dot_general(
        gathered_q, item_embeddings, (((1,), (1,)), ((), ())), preferred_element_type=jnp.float32
    ).reshape(panel, blocks_here, blk)
    target = jnp.exp(teach_local - lse_t[:, None, None])

    masked = jnp.where(valid, scores, -jnp.inf)
    m_part = jnp.max(masked, axis=(1, 2))
    l_part = jnp.sum(jnp.where(valid, jnp.exp(scores - m_part[:, None, None]), 0.0), axis=(1, 2))
    d_part = jnp.sum(jnp.where(valid, target * (teach_local - scores), 0.0), axis=(1, 2))
    stacked = jnp.stack([m_part, l_part, d_part])
    parts = lax.all_to_all(
        jnp.broadcast_to(stacked[None], (nitem,) + stacked.shape), ITEM, 0, 0, tiled=False
    )
    m_all, l_all, d_all = parts[:, 0], parts[:, 1], parts[:, 2]
    m_s = jnp.max(m_all, axis=0)
    lse_s = m_s + jnp.log(jnp.sum(l_all * jnp.exp(m_all - m_s[None, :]), axis=0))
    row_loss = jnp.sum(jnp.sum(d_all, axis=0) - lse_t + lse_s)

    probs = jnp.exp(scores - lse_s[:, None, None])
    coeff = jnp.where(valid, probs - target, 0.0).astype(jnp.bfloat16)
    dense_rows = coeff.reshape(panel, own_items)

    qg = jnp.dot(dense_rows, item_embeddings, preferred_element_type=jnp.float32)
    qg = qg.reshape(nitem, qdev, width)
    question_grads = jnp.sum(lax.all_to_all(qg, ITEM, 0, 0, tiled=False), axis=0)
    npb = lax.axis_size("pb")
    pieces = jnp.zeros((8, own_items), jnp.float32).at[0, :3].set(bf16_pieces(row_loss))
    payload = jnp.concatenate([dense_rows, pieces.astype(jnp.bfloat16)], axis=0)
    payload, all_q = lax.optimization_barrier((payload, all_q))
    got = lax.all_gather(payload, "pb", axis=0)
    item_grads = lax.dot_general(
        got[:, :panel], all_q, (((0, 1), (0, 1)), ((), ())), preferred_element_type=jnp.float32
    )
    loss_parts = got[:, panel, :3].astype(jnp.float32)
    total = jnp.sum(loss_parts[:, 0] + loss_parts[:, 1] + loss_parts[:, 2])
    loss = total / (panel * npb)
    return (loss, question_grads, item_grads)


def solution(mesh):
    npb, nitem = mesh.devices.shape
    ncore = 2
    nz = 8 if nitem % (8 * ncore) == 0 else 1
    fine = Mesh(mesh.devices.reshape(npb, nitem // (nz * ncore), nz, ncore), ("pb",) + ITEM)
    qspec = ("pb",) + ITEM
    return jax.shard_map(
        shards,
        mesh=fine,
        in_specs=(
            P(qspec, None),
            P(ITEM, None),
            P(qspec, None),
            P(qspec, None, None),
        ),
        out_specs=(P(), P(qspec, None), P(ITEM, None)),
        check_vma=False,
    )
```

```python
import jax
import jax.numpy as jnp
from jax import lax
from jax.sharding import Mesh, PartitionSpec as P


ITEM = ("y", "z", "c")


def row_lse(values):
    top = jnp.max(values, axis=1)
    return top + jnp.log(jnp.sum(jnp.exp(values - top[:, None]), axis=1))


def bf16_pieces(x):
    hi = lax.reduce_precision(x, exponent_bits=8, mantissa_bits=7)
    rest = x - hi
    mid = lax.reduce_precision(rest, exponent_bits=8, mantissa_bits=7)
    lo = lax.reduce_precision(rest - mid, exponent_bits=8, mantissa_bits=7)
    return jnp.stack([hi, mid, lo], axis=-1)


def shards(questions, item_embeddings, block_ids, teacher_scores):
    qdev, width = questions.shape
    slots = block_ids.shape[1]
    blk = teacher_scores.shape[2]
    own_items = item_embeddings.shape[0]
    blocks_here = own_items // blk
    nitem = lax.axis_size(ITEM)
    nblk = nitem * blocks_here
    panel = qdev * nitem
    base = lax.axis_index(ITEM) * blocks_here

    named = block_ids[:, :, None] == jnp.arange(nblk, dtype=jnp.int32)[None, None, :]
    routed = jnp.einsum(
        "qjb,qjk->bqk",
        named.astype(jnp.bfloat16),
        teacher_scores,
        preferred_element_type=jnp.float32,
    ).astype(jnp.bfloat16)
    routed = routed.reshape(nitem, blocks_here, qdev, blk).transpose(0, 2, 1, 3)
    routed = routed.reshape(nitem, qdev, own_items)

    ncore = lax.axis_size("c")
    nchip = nitem // ncore
    mask = jnp.any(named, axis=1).astype(jnp.bfloat16).reshape(qdev, nchip, ncore * blocks_here)
    lse_own = bf16_pieces(row_lse(teacher_scores.astype(jnp.float32).reshape(qdev, slots * blk)))
    lse_own = lse_own.astype(jnp.bfloat16)
    nmask = ncore * blocks_here
    pad = -(-(nmask + 3) // 128) * 128 - nmask - 3
    tail = jnp.concatenate(
        [
            mask.transpose(1, 0, 2),
            jnp.broadcast_to(lse_own[None], (nchip, qdev, 3)),
            jnp.zeros((nchip, qdev, pad), jnp.bfloat16),
        ],
        axis=2,
    )
    routed = routed.reshape(nchip, ncore, qdev, own_items).transpose(0, 2, 1, 3)
    routed = routed.reshape(nchip, qdev, ncore * own_items)
    send = jnp.concatenate(
        [jnp.broadcast_to(questions[None], (nchip, qdev, width)), routed, tail], axis=2
    )
    recv = lax.all_to_all(send, ("y", "z"), 0, 0, tiled=False)
    per_core = []
    for core in range(ncore):
        t0 = width + core * own_items
        per_core.append(
            jnp.concatenate(
                [
                    recv[:, :, :width],
                    recv[:, :, t0 : t0 + own_items],
                    recv[:, :, width + ncore * own_items :],
                ],
                axis=2,
            )
        )
    recv = lax.all_to_all(jnp.stack(per_core), "c", 0, 0, tiled=False)
    recv = recv.transpose(1, 0, 2, 3).reshape(panel, -1)
    my_core = lax.axis_index("c")
    gathered_q = recv[:, :width]
    teach_local = recv[:, width : width + own_items]
    teach_local = teach_local.reshape(panel, blocks_here, blk).astype(jnp.float32)
    tail0 = width + own_items
    valid = lax.dynamic_slice_in_dim(recv, tail0 + my_core * blocks_here, blocks_here, axis=1)
    valid = (valid > 0.5)[:, :, None]
    lse_parts = recv[:, tail0 + nmask : tail0 + nmask + 3]
    lse_parts = lse_parts.astype(jnp.float32)
    lse_t = lse_parts[:, 0] + lse_parts[:, 1] + lse_parts[:, 2]
    all_q = lax.all_gather(gathered_q, "pb", axis=0)

    scores = lax.dot_general(
        gathered_q, item_embeddings, (((1,), (1,)), ((), ())), preferred_element_type=jnp.float32
    ).reshape(panel, blocks_here, blk)
    target = jnp.exp(teach_local - lse_t[:, None, None])

    masked = jnp.where(valid, scores, -jnp.inf)
    m_part = jnp.max(masked, axis=(1, 2))
    l_part = jnp.sum(jnp.where(valid, jnp.exp(scores - m_part[:, None, None]), 0.0), axis=(1, 2))
    d_part = jnp.sum(jnp.where(valid, target * (teach_local - scores), 0.0), axis=(1, 2))
    stacked = jnp.stack([m_part, l_part, d_part])
    parts = lax.all_to_all(
        jnp.broadcast_to(stacked[None], (nitem,) + stacked.shape), ITEM, 0, 0, tiled=False
    )
    m_all, l_all, d_all = parts[:, 0], parts[:, 1], parts[:, 2]
    m_s = jnp.max(m_all, axis=0)
    lse_s = m_s + jnp.log(jnp.sum(l_all * jnp.exp(m_all - m_s[None, :]), axis=0))
    row_loss = jnp.sum(jnp.sum(d_all, axis=0) - lse_t + lse_s)

    probs = jnp.exp(scores - lse_s[:, None, None])
    coeff = jnp.where(valid, probs - target, 0.0).astype(jnp.bfloat16)
    dense_rows = coeff.reshape(panel, own_items)

    qg = jnp.dot(dense_rows, item_embeddings, preferred_element_type=jnp.float32)
    qg = qg.reshape(nitem, qdev, width)
    question_grads = jnp.sum(lax.all_to_all(qg, ITEM, 0, 0, tiled=False), axis=0)
    npb = lax.axis_size("pb")
    pieces = jnp.zeros((8, own_items), jnp.float32).at[0, :3].set(bf16_pieces(row_loss))
    payload = jnp.concatenate([dense_rows, pieces.astype(jnp.bfloat16)], axis=0)
    payload, all_q = lax.optimization_barrier((payload, all_q))
    got = lax.all_gather(payload, "pb", axis=0)
    item_grads = lax.dot_general(
        got[:, :panel], all_q, (((0, 1), (0, 1)), ((), ())), preferred_element_type=jnp.float32
    )
    loss_parts = got[:, panel, :3].astype(jnp.float32)
    total = jnp.sum(loss_parts[:, 0] + loss_parts[:, 1] + loss_parts[:, 2])
    loss = total / (panel * npb)
    return (loss, question_grads, item_grads)


def solution(mesh):
    npb, nitem = mesh.devices.shape
    ncore = 2
    nz = 8 if nitem % (8 * ncore) == 0 else 1
    fine = Mesh(mesh.devices.reshape(npb, nitem // (nz * ncore), nz, ncore), ("pb",) + ITEM)
    qspec = ("pb",) + ITEM
    return jax.shard_map(
        shards,
        mesh=fine,
        in_specs=(
            P(qspec, None),
            P(ITEM, None),
            P(qspec, None),
            P(qspec, None, None),
        ),
        out_specs=(P(), P(qspec, None), P(ITEM, None)),
        check_vma=False,
    )
```

```python
import jax
import jax.numpy as jnp
from jax import lax
from jax.sharding import Mesh, PartitionSpec as P


ITEM = ("y", "z", "c")


def row_lse(values):
    top = jnp.max(values, axis=1)
    return top + jnp.log(jnp.sum(jnp.exp(values - top[:, None]), axis=1))


def bf16_pieces(x):
    hi = lax.reduce_precision(x, exponent_bits=8, mantissa_bits=7)
    rest = x - hi
    mid = lax.reduce_precision(rest, exponent_bits=8, mantissa_bits=7)
    lo = lax.reduce_precision(rest - mid, exponent_bits=8, mantissa_bits=7)
    return jnp.stack([hi, mid, lo], axis=-1)


def shards(questions, item_embeddings, block_ids, teacher_scores):
    qdev, width = questions.shape
    slots = block_ids.shape[1]
    blk = teacher_scores.shape[2]
    own_items = item_embeddings.shape[0]
    blocks_here = own_items // blk
    nitem = lax.axis_size(ITEM)
    nblk = nitem * blocks_here
    panel = qdev * nitem
    base = lax.axis_index(ITEM) * blocks_here

    named = block_ids[:, :, None] == jnp.arange(nblk, dtype=jnp.int32)[None, None, :]
    routed = jnp.einsum(
        "qjb,qjk->bqk",
        named.astype(jnp.bfloat16),
        teacher_scores,
        preferred_element_type=jnp.float32,
    ).astype(jnp.bfloat16)
    routed = routed.reshape(nitem, blocks_here, qdev, blk).transpose(0, 2, 1, 3)
    routed = routed.reshape(nitem, qdev, own_items)

    ncore = lax.axis_size("c")
    nchip = nitem // ncore
    mask = jnp.any(named, axis=1).astype(jnp.bfloat16).reshape(qdev, nchip, ncore * blocks_here)
    lse_own = bf16_pieces(row_lse(teacher_scores.astype(jnp.float32).reshape(qdev, slots * blk)))
    lse_own = lse_own.astype(jnp.bfloat16)
    nmask = ncore * blocks_here
    pad = -(-(nmask + 3) // 128) * 128 - nmask - 3
    tail = jnp.concatenate(
        [
            mask.transpose(1, 0, 2),
            jnp.broadcast_to(lse_own[None], (nchip, qdev, 3)),
            jnp.zeros((nchip, qdev, pad), jnp.bfloat16),
        ],
        axis=2,
    )
    routed = routed.reshape(nchip, ncore, qdev, own_items).transpose(0, 2, 1, 3)
    routed = routed.reshape(nchip, qdev, ncore * own_items)
    send = jnp.concatenate(
        [jnp.broadcast_to(questions[None], (nchip, qdev, width)), routed, tail], axis=2
    )
    recv = lax.all_to_all(send, ("y", "z"), 0, 0, tiled=False)
    per_core = []
    for core in range(ncore):
        t0 = width + core * own_items
        per_core.append(
            jnp.concatenate(
                [
                    recv[:, :, :width],
                    recv[:, :, t0 : t0 + own_items],
                    recv[:, :, width + ncore * own_items :],
                ],
                axis=2,
            )
        )
    recv = lax.all_to_all(jnp.stack(per_core), "c", 0, 0, tiled=False)
    recv = recv.transpose(1, 0, 2, 3).reshape(panel, -1)
    my_core = lax.axis_index("c")
    gathered_q = recv[:, :width]
    teach_local = recv[:, width : width + own_items]
    teach_local = teach_local.reshape(panel, blocks_here, blk).astype(jnp.float32)
    tail0 = width + own_items
    valid = lax.dynamic_slice_in_dim(recv, tail0 + my_core * blocks_here, blocks_here, axis=1)
    valid = (valid > 0.5)[:, :, None]
    lse_parts = recv[:, tail0 + nmask : tail0 + nmask + 3]
    lse_parts = lse_parts.astype(jnp.float32)
    lse_t = lse_parts[:, 0] + lse_parts[:, 1] + lse_parts[:, 2]
    all_q = lax.all_gather(gathered_q, "pb", axis=0)

    scores = lax.dot_general(
        gathered_q, item_embeddings, (((1,), (1,)), ((), ())), preferred_element_type=jnp.float32
    ).reshape(panel, blocks_here, blk)
    target = jnp.exp(teach_local - lse_t[:, None, None])

    masked = jnp.where(valid, scores, -jnp.inf)
    m_part = jnp.max(masked, axis=(1, 2))
    l_part = jnp.sum(jnp.where(valid, jnp.exp(scores - m_part[:, None, None]), 0.0), axis=(1, 2))
    d_part = jnp.sum(jnp.where(valid, target * (teach_local - scores), 0.0), axis=(1, 2))
    stacked = jnp.stack([m_part, l_part, d_part])
    parts = lax.all_to_all(
        jnp.broadcast_to(stacked[None], (nchip,) + stacked.shape), ("y", "z"), 0, 0, tiled=False
    )
    parts = lax.all_to_all(
        jnp.broadcast_to(parts[None], (ncore,) + parts.shape), "c", 0, 0, tiled=False
    ).reshape((nitem,) + stacked.shape)
    m_all, l_all, d_all = parts[:, 0], parts[:, 1], parts[:, 2]
    m_s = jnp.max(m_all, axis=0)
    lse_s = m_s + jnp.log(jnp.sum(l_all * jnp.exp(m_all - m_s[None, :]), axis=0))
    row_loss = jnp.sum(jnp.sum(d_all, axis=0) - lse_t + lse_s)

    probs = jnp.exp(scores - lse_s[:, None, None])
    coeff = jnp.where(valid, probs - target, 0.0).astype(jnp.bfloat16)
    dense_rows = coeff.reshape(panel, own_items)

    qg = jnp.dot(dense_rows, item_embeddings, preferred_element_type=jnp.float32)
    qg = qg.reshape(nitem, qdev, width)
    question_grads = jnp.sum(lax.all_to_all(qg, ITEM, 0, 0, tiled=False), axis=0)
    npb = lax.axis_size("pb")
    pieces = jnp.zeros((8, own_items), jnp.float32).at[0, :3].set(bf16_pieces(row_loss))
    payload = jnp.concatenate([dense_rows, pieces.astype(jnp.bfloat16)], axis=0)
    payload, all_q = lax.optimization_barrier((payload, all_q))
    got = lax.all_gather(payload, "pb", axis=0)
    item_grads = lax.dot_general(
        got[:, :panel], all_q, (((0, 1), (0, 1)), ((), ())), preferred_element_type=jnp.float32
    )
    loss_parts = got[:, panel, :3].astype(jnp.float32)
    total = jnp.sum(loss_parts[:, 0] + loss_parts[:, 1] + loss_parts[:, 2])
    loss = total / (panel * npb)
    return (loss, question_grads, item_grads)


def solution(mesh):
    npb, nitem = mesh.devices.shape
    ncore = 2
    nz = 8 if nitem % (8 * ncore) == 0 else 1
    fine = Mesh(mesh.devices.reshape(npb, nitem // (nz * ncore), nz, ncore), ("pb",) + ITEM)
    qspec = ("pb",) + ITEM
    return jax.shard_map(
        shards,
        mesh=fine,
        in_specs=(
            P(qspec, None),
            P(ITEM, None),
            P(qspec, None),
            P(qspec, None, None),
        ),
        out_specs=(P(), P(qspec, None), P(ITEM, None)),
        check_vma=False,
    )
```

```python
import jax
import jax.numpy as jnp
from jax import lax
from jax.sharding import Mesh, PartitionSpec as P


ITEM = ("y", "z", "c")


def row_lse(values):
    top = jnp.max(values, axis=1)
    return top + jnp.log(jnp.sum(jnp.exp(values - top[:, None]), axis=1))


def bf16_pieces(x):
    hi = lax.reduce_precision(x, exponent_bits=8, mantissa_bits=7)
    rest = x - hi
    mid = lax.reduce_precision(rest, exponent_bits=8, mantissa_bits=7)
    lo = lax.reduce_precision(rest - mid, exponent_bits=8, mantissa_bits=7)
    return jnp.stack([hi, mid, lo], axis=-1)


def shards(questions, item_embeddings, block_ids, teacher_scores):
    qdev, width = questions.shape
    slots = block_ids.shape[1]
    blk = teacher_scores.shape[2]
    own_items = item_embeddings.shape[0]
    blocks_here = own_items // blk
    nitem = lax.axis_size(ITEM)
    nblk = nitem * blocks_here
    panel = qdev * nitem
    base = lax.axis_index(ITEM) * blocks_here

    named = block_ids[:, :, None] == jnp.arange(nblk, dtype=jnp.int32)[None, None, :]
    routed = jnp.einsum(
        "qjb,qjk->bqk",
        named.astype(jnp.bfloat16),
        teacher_scores,
        preferred_element_type=jnp.float32,
    ).astype(jnp.bfloat16)
    routed = routed.reshape(nitem, blocks_here, qdev, blk).transpose(0, 2, 1, 3)
    routed = routed.reshape(nitem, qdev, own_items)

    ncore = lax.axis_size("c")
    nchip = nitem // ncore
    mask = jnp.any(named, axis=1).astype(jnp.bfloat16).reshape(qdev, nchip, ncore * blocks_here)
    lse_own = bf16_pieces(row_lse(teacher_scores.astype(jnp.float32).reshape(qdev, slots * blk)))
    lse_own = lse_own.astype(jnp.bfloat16)
    nmask = ncore * blocks_here
    pad = -(-(nmask + 3) // 128) * 128 - nmask - 3
    tail = jnp.concatenate(
        [
            mask.transpose(1, 0, 2),
            jnp.broadcast_to(lse_own[None], (nchip, qdev, 3)),
            jnp.zeros((nchip, qdev, pad), jnp.bfloat16),
        ],
        axis=2,
    )
    routed = routed.reshape(nchip, ncore, qdev, own_items).transpose(0, 2, 1, 3)
    routed = routed.reshape(nchip, qdev, ncore * own_items)
    send = jnp.concatenate(
        [jnp.broadcast_to(questions[None], (nchip, qdev, width)), routed, tail], axis=2
    )
    recv = lax.all_to_all(send, ("y", "z"), 0, 0, tiled=False)
    per_core = []
    for core in range(ncore):
        t0 = width + core * own_items
        per_core.append(
            jnp.concatenate(
                [
                    recv[:, :, :width],
                    recv[:, :, t0 : t0 + own_items],
                    recv[:, :, width + ncore * own_items :],
                ],
                axis=2,
            )
        )
    recv = lax.all_to_all(jnp.stack(per_core), "c", 0, 0, tiled=False)
    recv = recv.transpose(1, 0, 2, 3).reshape(panel, -1)
    my_core = lax.axis_index("c")
    gathered_q = recv[:, :width]
    teach_local = recv[:, width : width + own_items]
    teach_local = teach_local.reshape(panel, blocks_here, blk).astype(jnp.float32)
    tail0 = width + own_items
    valid = lax.dynamic_slice_in_dim(recv, tail0 + my_core * blocks_here, blocks_here, axis=1)
    valid = (valid > 0.5)[:, :, None]
    lse_parts = recv[:, tail0 + nmask : tail0 + nmask + 3]
    lse_parts = lse_parts.astype(jnp.float32)
    lse_t = lse_parts[:, 0] + lse_parts[:, 1] + lse_parts[:, 2]
    half = panel // ncore
    q_half = lax.all_gather(
        lax.dynamic_slice_in_dim(gathered_q, my_core * half, half, axis=0), "pb", axis=0
    )

    scores = lax.dot_general(
        gathered_q, item_embeddings, (((1,), (1,)), ((), ())), preferred_element_type=jnp.float32
    ).reshape(panel, blocks_here, blk)
    target = jnp.exp(teach_local - lse_t[:, None, None])

    masked = jnp.where(valid, scores, -jnp.inf)
    m_part = jnp.max(masked, axis=(1, 2))
    l_part = jnp.sum(jnp.where(valid, jnp.exp(scores - m_part[:, None, None]), 0.0), axis=(1, 2))
    d_part = jnp.sum(jnp.where(valid, target * (teach_local - scores), 0.0), axis=(1, 2))
    stacked = jnp.stack([m_part, l_part, d_part])
    parts = lax.all_to_all(
        jnp.broadcast_to(stacked[None], (nchip,) + stacked.shape), ("y", "z"), 0, 0, tiled=False
    )
    parts = lax.all_to_all(
        jnp.broadcast_to(parts[None], (ncore,) + parts.shape), "c", 0, 0, tiled=False
    ).reshape((nitem,) + stacked.shape)
    m_all, l_all, d_all = parts[:, 0], parts[:, 1], parts[:, 2]
    m_s = jnp.max(m_all, axis=0)
    lse_s = m_s + jnp.log(jnp.sum(l_all * jnp.exp(m_all - m_s[None, :]), axis=0))
    row_loss = jnp.sum(jnp.sum(d_all, axis=0) - lse_t + lse_s)

    probs = jnp.exp(scores - lse_s[:, None, None])
    coeff = jnp.where(valid, probs - target, 0.0).astype(jnp.bfloat16)
    dense_rows = coeff.reshape(panel, own_items)

    qg = jnp.dot(dense_rows, item_embeddings, preferred_element_type=jnp.float32)
    qg = qg.reshape(nchip, ncore, qdev, width).transpose(1, 0, 2, 3)
    qg = jnp.sum(lax.all_to_all(qg, "c", 0, 0, tiled=False), axis=0)
    question_grads = jnp.sum(lax.all_to_all(qg, ("y", "z"), 0, 0, tiled=False), axis=0)
    npb = lax.axis_size("pb")
    pieces = jnp.zeros((8, own_items), jnp.float32).at[0, :3].set(bf16_pieces(row_loss))
    payload = jnp.concatenate([dense_rows, pieces.astype(jnp.bfloat16)], axis=0)
    all_q = lax.all_to_all(
        jnp.broadcast_to(q_half[None], (ncore,) + q_half.shape), "c", 0, 0, tiled=False
    )
    payload, all_q = lax.optimization_barrier((payload, all_q))
    got = lax.all_gather(payload, "pb", axis=0)
    coeff_all = got[:, :panel].reshape(npb, ncore, half, own_items)
    item_grads = lax.dot_general(
        coeff_all, all_q, (((0, 1, 2), (1, 0, 2)), ((), ())), preferred_element_type=jnp.float32
    )
    loss_parts = got[:, panel, :3].astype(jnp.float32)
    total = jnp.sum(loss_parts[:, 0] + loss_parts[:, 1] + loss_parts[:, 2])
    loss = total / (panel * npb)
    return (loss, question_grads, item_grads)


def solution(mesh):
    npb, nitem = mesh.devices.shape
    ncore = 2
    nz = 8 if nitem % (8 * ncore) == 0 else 1
    fine = Mesh(mesh.devices.reshape(npb, nitem // (nz * ncore), nz, ncore), ("pb",) + ITEM)
    qspec = ("pb",) + ITEM
    return jax.shard_map(
        shards,
        mesh=fine,
        in_specs=(
            P(qspec, None),
            P(ITEM, None),
            P(qspec, None),
            P(qspec, None, None),
        ),
        out_specs=(P(), P(qspec, None), P(ITEM, None)),
        check_vma=False,
    )
```

```python
import jax
import jax.numpy as jnp
from jax import lax
from jax.sharding import Mesh, PartitionSpec as P


ITEM = ("y", "z", "c")


def row_lse(values):
    top = jnp.max(values, axis=1)
    return top + jnp.log(jnp.sum(jnp.exp(values - top[:, None]), axis=1))


def bf16_pieces(x):
    hi = lax.reduce_precision(x, exponent_bits=8, mantissa_bits=7)
    rest = x - hi
    mid = lax.reduce_precision(rest, exponent_bits=8, mantissa_bits=7)
    lo = lax.reduce_precision(rest - mid, exponent_bits=8, mantissa_bits=7)
    return jnp.stack([hi, mid, lo], axis=-1)


def shards(questions, item_embeddings, block_ids, teacher_scores):
    qdev, width = questions.shape
    slots = block_ids.shape[1]
    blk = teacher_scores.shape[2]
    own_items = item_embeddings.shape[0]
    blocks_here = own_items // blk
    nitem = lax.axis_size(ITEM)
    nblk = nitem * blocks_here
    panel = qdev * nitem
    base = lax.axis_index(ITEM) * blocks_here

    named = block_ids[:, :, None] == jnp.arange(nblk, dtype=jnp.int32)[None, None, :]
    routed = jnp.einsum(
        "qjb,qjk->bqk",
        named.astype(jnp.bfloat16),
        teacher_scores,
        preferred_element_type=jnp.float32,
    ).astype(jnp.bfloat16)
    routed = routed.reshape(nitem, blocks_here, qdev, blk).transpose(0, 2, 1, 3)
    routed = routed.reshape(nitem, qdev, own_items)

    ncore = lax.axis_size("c")
    nchip = nitem // ncore
    mask = jnp.any(named, axis=1).astype(jnp.bfloat16).reshape(qdev, nchip, ncore * blocks_here)
    lse_own = bf16_pieces(row_lse(teacher_scores.astype(jnp.float32).reshape(qdev, slots * blk)))
    lse_own = lse_own.astype(jnp.bfloat16)
    nmask = ncore * blocks_here
    pad = -(-(nmask + 3) // 128) * 128 - nmask - 3
    tail = jnp.concatenate(
        [
            mask.transpose(1, 0, 2),
            jnp.broadcast_to(lse_own[None], (nchip, qdev, 3)),
            jnp.zeros((nchip, qdev, pad), jnp.bfloat16),
        ],
        axis=2,
    )
    routed = routed.reshape(nchip, ncore, qdev, own_items).transpose(0, 2, 1, 3)
    routed = routed.reshape(nchip, qdev, ncore * own_items)
    send = jnp.concatenate(
        [jnp.broadcast_to(questions[None], (nchip, qdev, width)), routed, tail], axis=2
    )
    recv = lax.all_to_all(send, ("y", "z"), 0, 0, tiled=False)
    per_core = []
    for core in range(ncore):
        t0 = width + core * own_items
        per_core.append(
            jnp.concatenate(
                [
                    recv[:, :, :width],
                    recv[:, :, t0 : t0 + own_items],
                    recv[:, :, width + ncore * own_items :],
                ],
                axis=2,
            )
        )
    recv = lax.all_to_all(jnp.stack(per_core), "c", 0, 0, tiled=False)
    recv = recv.transpose(1, 0, 2, 3).reshape(panel, -1)
    my_core = lax.axis_index("c")
    gathered_q = recv[:, :width]
    teach_local = recv[:, width : width + own_items]
    teach_local = teach_local.reshape(panel, blocks_here, blk).astype(jnp.float32)
    tail0 = width + own_items
    valid = lax.dynamic_slice_in_dim(recv, tail0 + my_core * blocks_here, blocks_here, axis=1)
    valid = (valid > 0.5)[:, :, None]
    lse_parts = recv[:, tail0 + nmask : tail0 + nmask + 3]
    lse_parts = lse_parts.astype(jnp.float32)
    lse_t = lse_parts[:, 0] + lse_parts[:, 1] + lse_parts[:, 2]
    half = panel // ncore
    q_half = lax.all_gather(
        lax.dynamic_slice_in_dim(gathered_q, my_core * half, half, axis=0), "pb", axis=0
    )

    scores = lax.dot_general(
        gathered_q, item_embeddings, (((1,), (1,)), ((), ())), preferred_element_type=jnp.float32
    ).reshape(panel, blocks_here, blk)
    target = jnp.exp(teach_local - lse_t[:, None, None])

    masked = jnp.where(valid, scores, -jnp.inf)
    m_part = jnp.max(masked, axis=(1, 2))
    l_part = jnp.sum(jnp.where(valid, jnp.exp(scores - m_part[:, None, None]), 0.0), axis=(1, 2))
    d_part = jnp.sum(jnp.where(valid, target * (teach_local - scores), 0.0), axis=(1, 2))
    stacked = jnp.stack([m_part, l_part, d_part])
    parts = lax.all_to_all(
        jnp.broadcast_to(stacked[None], (nchip,) + stacked.shape), ("y", "z"), 0, 0, tiled=False
    )
    parts = lax.all_to_all(
        jnp.broadcast_to(parts[None], (ncore,) + parts.shape), "c", 0, 0, tiled=False
    ).reshape((nitem,) + stacked.shape)
    m_all, l_all, d_all = parts[:, 0], parts[:, 1], parts[:, 2]
    m_s = jnp.max(m_all, axis=0)
    lse_s = m_s + jnp.log(jnp.sum(l_all * jnp.exp(m_all - m_s[None, :]), axis=0))
    row_loss = jnp.sum(jnp.sum(d_all, axis=0) - lse_t + lse_s)

    probs = jnp.exp(scores - lse_s[:, None, None])
    coeff = jnp.where(valid, probs - target, 0.0).astype(jnp.bfloat16)
    dense_rows = coeff.reshape(panel, own_items)

    qg = jnp.dot(dense_rows, item_embeddings, preferred_element_type=jnp.float32)
    qg = qg.reshape(nchip, ncore, qdev, width).transpose(1, 0, 2, 3)
    qg = jnp.sum(lax.all_to_all(qg, "c", 0, 0, tiled=False), axis=0)
    question_grads = jnp.sum(lax.all_to_all(qg, ("y", "z"), 0, 0, tiled=False), axis=0)
    npb = lax.axis_size("pb")
    pieces = jnp.zeros((8, own_items), jnp.float32).at[0, :3].set(bf16_pieces(row_loss))
    payload = jnp.concatenate([dense_rows, pieces.astype(jnp.bfloat16)], axis=0)
    payload, q_half = lax.optimization_barrier((payload, q_half))
    other_half = lax.ppermute(q_half, "c", [(0, 1), (1, 0)])
    got = lax.all_gather(payload, "pb", axis=0)
    coeff_all = got[:, :panel].reshape(npb, ncore, half, own_items)
    contract = (((0, 1), (0, 1)), ((), ()))
    item_grads = lax.dot_general(
        coeff_all[:, my_core], q_half, contract, preferred_element_type=jnp.float32
    ) + lax.dot_general(
        coeff_all[:, 1 - my_core], other_half, contract, preferred_element_type=jnp.float32
    )
    loss_parts = got[:, panel, :3].astype(jnp.float32)
    total = jnp.sum(loss_parts[:, 0] + loss_parts[:, 1] + loss_parts[:, 2])
    loss = total / (panel * npb)
    return (loss, question_grads, item_grads)


def solution(mesh):
    npb, nitem = mesh.devices.shape
    ncore = 2
    nz = 8 if nitem % (8 * ncore) == 0 else 1
    fine = Mesh(mesh.devices.reshape(npb, nitem // (nz * ncore), nz, ncore), ("pb",) + ITEM)
    qspec = ("pb",) + ITEM
    return jax.shard_map(
        shards,
        mesh=fine,
        in_specs=(
            P(qspec, None),
            P(ITEM, None),
            P(qspec, None),
            P(qspec, None, None),
        ),
        out_specs=(P(), P(qspec, None), P(ITEM, None)),
        check_vma=False,
    )
```

```python
import jax
import jax.numpy as jnp
from jax import lax
from jax.sharding import Mesh, PartitionSpec as P


ITEM = ("y", "z", "c")


def row_lse(values):
    top = jnp.max(values, axis=1)
    return top + jnp.log(jnp.sum(jnp.exp(values - top[:, None]), axis=1))


def bf16_pieces(x):
    hi = lax.reduce_precision(x, exponent_bits=8, mantissa_bits=7)
    rest = x - hi
    mid = lax.reduce_precision(rest, exponent_bits=8, mantissa_bits=7)
    lo = lax.reduce_precision(rest - mid, exponent_bits=8, mantissa_bits=7)
    return jnp.stack([hi, mid, lo], axis=-1)


def shards(questions, item_embeddings, block_ids, teacher_scores):
    qdev, width = questions.shape
    slots = block_ids.shape[1]
    blk = teacher_scores.shape[2]
    own_items = item_embeddings.shape[0]
    blocks_here = own_items // blk
    nitem = lax.axis_size(ITEM)
    nblk = nitem * blocks_here
    panel = qdev * nitem
    base = lax.axis_index(ITEM) * blocks_here

    named = block_ids[:, :, None] == jnp.arange(nblk, dtype=jnp.int32)[None, None, :]
    routed = jnp.einsum(
        "qjb,qjk->bqk",
        named.astype(jnp.bfloat16),
        teacher_scores,
        preferred_element_type=jnp.float32,
    ).astype(jnp.bfloat16)
    routed = routed.reshape(nitem, blocks_here, qdev, blk).transpose(0, 2, 1, 3)
    routed = routed.reshape(nitem, qdev, own_items)

    ncore = lax.axis_size("c")
    nchip = nitem // ncore
    mask = jnp.any(named, axis=1).astype(jnp.bfloat16).reshape(qdev, nchip, ncore * blocks_here)
    lse_own = bf16_pieces(row_lse(teacher_scores.astype(jnp.float32).reshape(qdev, slots * blk)))
    lse_own = lse_own.astype(jnp.bfloat16)
    nmask = ncore * blocks_here
    pad = -(-(nmask + 3) // 128) * 128 - nmask - 3
    tail = jnp.concatenate(
        [
            mask.transpose(1, 0, 2),
            jnp.broadcast_to(lse_own[None], (nchip, qdev, 3)),
            jnp.zeros((nchip, qdev, pad), jnp.bfloat16),
        ],
        axis=2,
    )
    routed = routed.reshape(nchip, ncore, qdev, own_items).transpose(0, 2, 1, 3)
    routed = routed.reshape(nchip, qdev, ncore * own_items)
    send = jnp.concatenate(
        [jnp.broadcast_to(questions[None], (nchip, qdev, width)), routed, tail], axis=2
    )
    recv = lax.all_to_all(send, ("y", "z"), 0, 0, tiled=False)
    per_core = []
    for core in range(ncore):
        t0 = width + core * own_items
        per_core.append(
            jnp.concatenate(
                [
                    recv[:, :, :width],
                    recv[:, :, t0 : t0 + own_items],
                    recv[:, :, width + ncore * own_items :],
                ],
                axis=2,
            )
        )
    recv = lax.all_to_all(jnp.stack(per_core), "c", 0, 0, tiled=False)
    recv = recv.transpose(1, 0, 2, 3).reshape(panel, -1)
    my_core = lax.axis_index("c")
    gathered_q = recv[:, :width]
    teach_local = recv[:, width : width + own_items]
    teach_local = teach_local.reshape(panel, blocks_here, blk).astype(jnp.float32)
    tail0 = width + own_items
    valid = lax.dynamic_slice_in_dim(recv, tail0 + my_core * blocks_here, blocks_here, axis=1)
    valid = (valid > 0.5)[:, :, None]
    lse_parts = recv[:, tail0 + nmask : tail0 + nmask + 3]
    lse_parts = lse_parts.astype(jnp.float32)
    lse_t = lse_parts[:, 0] + lse_parts[:, 1] + lse_parts[:, 2]
    half = panel // ncore
    q_half = lax.all_gather(
        lax.dynamic_slice_in_dim(gathered_q, my_core * half, half, axis=0), "pb", axis=0
    )

    scores = lax.dot_general(
        gathered_q, item_embeddings, (((1,), (1,)), ((), ())), preferred_element_type=jnp.float32
    ).reshape(panel, blocks_here, blk)
    target = jnp.exp(teach_local - lse_t[:, None, None])

    masked = jnp.where(valid, scores, -jnp.inf)
    m_part = jnp.max(masked, axis=(1, 2))
    l_part = jnp.sum(jnp.where(valid, jnp.exp(scores - m_part[:, None, None]), 0.0), axis=(1, 2))
    d_part = jnp.sum(jnp.where(valid, target * (teach_local - scores), 0.0), axis=(1, 2))
    stacked = jnp.stack([m_part, l_part, d_part])
    parts = lax.all_to_all(
        jnp.broadcast_to(stacked[None], (nchip,) + stacked.shape), ("y", "z"), 0, 0, tiled=False
    )
    parts = lax.all_to_all(
        jnp.broadcast_to(parts[None], (ncore,) + parts.shape), "c", 0, 0, tiled=False
    ).reshape((nitem,) + stacked.shape)
    m_all, l_all, d_all = parts[:, 0], parts[:, 1], parts[:, 2]
    m_s = jnp.max(m_all, axis=0)
    lse_s = m_s + jnp.log(jnp.sum(l_all * jnp.exp(m_all - m_s[None, :]), axis=0))
    row_loss = jnp.sum(jnp.sum(d_all, axis=0) - lse_t + lse_s)

    probs = jnp.exp(scores - lse_s[:, None, None])
    coeff = jnp.where(valid, probs - target, 0.0).astype(jnp.bfloat16)
    dense_rows = coeff.reshape(panel, own_items)

    qg = jnp.dot(dense_rows, item_embeddings, preferred_element_type=jnp.float32)
    qg = qg.reshape(nchip, ncore, qdev, width).transpose(1, 0, 2, 3)
    qg = jnp.sum(lax.all_to_all(qg, "c", 0, 0, tiled=False), axis=0)
    qg_parts = lax.all_to_all(qg, ("y", "z"), 0, 0, tiled=False)
    npb = lax.axis_size("pb")
    pieces = jnp.zeros((8, own_items), jnp.float32).at[0, :3].set(bf16_pieces(row_loss))
    payload = jnp.concatenate([dense_rows, pieces.astype(jnp.bfloat16)], axis=0)
    payload, q_half = lax.optimization_barrier((payload, q_half))
    other_half = lax.ppermute(q_half, "c", [(0, 1), (1, 0)])
    got = lax.all_gather(payload, "pb", axis=0)
    coeff_all = got[:, :panel].reshape(npb, ncore, half, own_items)
    contract = (((0, 1), (0, 1)), ((), ()))
    item_grads = lax.dot_general(
        coeff_all[:, my_core], q_half, contract, preferred_element_type=jnp.float32
    ) + lax.dot_general(
        coeff_all[:, 1 - my_core], other_half, contract, preferred_element_type=jnp.float32
    )
    qg_parts, item_grads = lax.optimization_barrier((qg_parts, item_grads))
    question_grads = jnp.sum(qg_parts, axis=0)
    loss_parts = got[:, panel, :3].astype(jnp.float32)
    total = jnp.sum(loss_parts[:, 0] + loss_parts[:, 1] + loss_parts[:, 2])
    loss = total / (panel * npb)
    return (loss, question_grads, item_grads)


def solution(mesh):
    npb, nitem = mesh.devices.shape
    ncore = 2
    nz = 8 if nitem % (8 * ncore) == 0 else 1
    fine = Mesh(mesh.devices.reshape(npb, nitem // (nz * ncore), nz, ncore), ("pb",) + ITEM)
    qspec = ("pb",) + ITEM
    return jax.shard_map(
        shards,
        mesh=fine,
        in_specs=(
            P(qspec, None),
            P(ITEM, None),
            P(qspec, None),
            P(qspec, None, None),
        ),
        out_specs=(P(), P(qspec, None), P(ITEM, None)),
        check_vma=False,
    )
```

```python
import jax
import jax.numpy as jnp
from jax import lax
from jax.sharding import Mesh, PartitionSpec as P


ITEM = ("y", "z", "c")


def row_lse(values):
    top = jnp.max(values, axis=1)
    return top + jnp.log(jnp.sum(jnp.exp(values - top[:, None]), axis=1))


def bf16_pieces(x):
    hi = lax.reduce_precision(x, exponent_bits=8, mantissa_bits=7)
    rest = x - hi
    mid = lax.reduce_precision(rest, exponent_bits=8, mantissa_bits=7)
    lo = lax.reduce_precision(rest - mid, exponent_bits=8, mantissa_bits=7)
    return jnp.stack([hi, mid, lo], axis=-1)


def shards(questions, item_embeddings, block_ids, teacher_scores):
    qdev, width = questions.shape
    slots = block_ids.shape[1]
    blk = teacher_scores.shape[2]
    own_items = item_embeddings.shape[0]
    blocks_here = own_items // blk
    nitem = lax.axis_size(ITEM)
    nblk = nitem * blocks_here
    panel = qdev * nitem
    base = lax.axis_index(ITEM) * blocks_here

    named = block_ids[:, :, None] == jnp.arange(nblk, dtype=jnp.int32)[None, None, :]
    routed = jnp.einsum(
        "qjb,qjk->bqk",
        named.astype(jnp.bfloat16),
        teacher_scores,
        preferred_element_type=jnp.float32,
    ).astype(jnp.bfloat16)
    routed = routed.reshape(nitem, blocks_here, qdev, blk).transpose(0, 2, 1, 3)
    routed = routed.reshape(nitem, qdev, own_items)

    ncore = lax.axis_size("c")
    nchip = nitem // ncore
    mask = jnp.any(named, axis=1).astype(jnp.bfloat16).reshape(qdev, nchip, ncore * blocks_here)
    lse_own = bf16_pieces(row_lse(teacher_scores.astype(jnp.float32).reshape(qdev, slots * blk)))
    lse_own = lse_own.astype(jnp.bfloat16)
    nmask = ncore * blocks_here
    pad = -(-(nmask + 3) // 128) * 128 - nmask - 3
    tail = jnp.concatenate(
        [
            mask.transpose(1, 0, 2),
            jnp.broadcast_to(lse_own[None], (nchip, qdev, 3)),
            jnp.zeros((nchip, qdev, pad), jnp.bfloat16),
        ],
        axis=2,
    )
    routed = routed.reshape(nchip, ncore, qdev, own_items).transpose(0, 2, 1, 3)
    routed = routed.reshape(nchip, qdev, ncore * own_items)
    send = jnp.concatenate(
        [jnp.broadcast_to(questions[None], (nchip, qdev, width)), routed, tail], axis=2
    )
    recv = lax.all_to_all(send, ("y", "z"), 0, 0, tiled=False)
    per_core = []
    for core in range(ncore):
        t0 = width + core * own_items
        per_core.append(
            jnp.concatenate(
                [
                    recv[:, :, :width],
                    recv[:, :, t0 : t0 + own_items],
                    recv[:, :, width + ncore * own_items :],
                ],
                axis=2,
            )
        )
    recv = lax.all_to_all(jnp.stack(per_core), "c", 0, 0, tiled=False)
    recv = recv.transpose(1, 0, 2, 3).reshape(panel, -1)
    my_core = lax.axis_index("c")
    gathered_q = recv[:, :width]
    teach_local = recv[:, width : width + own_items]
    teach_local = teach_local.reshape(panel, blocks_here, blk).astype(jnp.float32)
    tail0 = width + own_items
    valid = lax.dynamic_slice_in_dim(recv, tail0 + my_core * blocks_here, blocks_here, axis=1)
    valid = (valid > 0.5)[:, :, None]
    lse_parts = recv[:, tail0 + nmask : tail0 + nmask + 3]
    lse_parts = lse_parts.astype(jnp.float32)
    lse_t = lse_parts[:, 0] + lse_parts[:, 1] + lse_parts[:, 2]
    half = panel // ncore
    q_half = lax.all_gather(
        lax.dynamic_slice_in_dim(gathered_q, my_core * half, half, axis=0), "pb", axis=0
    )

    scores = lax.dot_general(
        gathered_q, item_embeddings, (((1,), (1,)), ((), ())), preferred_element_type=jnp.float32
    ).reshape(panel, blocks_here, blk)
    target = jnp.exp(teach_local - lse_t[:, None, None])

    masked = jnp.where(valid, scores, -jnp.inf)
    m_part = jnp.max(masked, axis=(1, 2))
    l_part = jnp.sum(jnp.where(valid, jnp.exp(scores - m_part[:, None, None]), 0.0), axis=(1, 2))
    d_part = jnp.sum(jnp.where(valid, target * (teach_local - scores), 0.0), axis=(1, 2))
    stacked = jnp.stack([m_part, l_part, d_part])
    parts = lax.all_to_all(
        jnp.broadcast_to(stacked[None], (nchip,) + stacked.shape), ("y", "z"), 0, 0, tiled=False
    )
    parts = lax.all_to_all(
        jnp.broadcast_to(parts[None], (ncore,) + parts.shape), "c", 0, 0, tiled=False
    ).reshape((nitem,) + stacked.shape)
    m_all, l_all, d_all = parts[:, 0], parts[:, 1], parts[:, 2]
    m_s = jnp.max(m_all, axis=0)
    lse_s = m_s + jnp.log(jnp.sum(l_all * jnp.exp(m_all - m_s[None, :]), axis=0))
    row_loss = jnp.sum(jnp.sum(d_all, axis=0) - lse_t + lse_s)

    probs = jnp.exp(scores - lse_s[:, None, None])
    coeff = jnp.where(valid, probs - target, 0.0).astype(jnp.bfloat16)
    dense_rows = coeff.reshape(panel, own_items)

    qg = jnp.dot(dense_rows, item_embeddings, preferred_element_type=jnp.float32)
    qg = qg.reshape(nchip, ncore, qdev, width)
    qg = qg[:, my_core] + lax.ppermute(qg[:, 1 - my_core], "c", [(0, 1), (1, 0)])
    qg_parts = lax.all_to_all(qg, ("y", "z"), 0, 0, tiled=False)
    npb = lax.axis_size("pb")
    pieces = jnp.zeros((8, own_items), jnp.float32).at[0, :3].set(bf16_pieces(row_loss))
    payload = jnp.concatenate([dense_rows, pieces.astype(jnp.bfloat16)], axis=0)
    payload, q_half = lax.optimization_barrier((payload, q_half))
    other_half = lax.ppermute(q_half, "c", [(0, 1), (1, 0)])
    got = lax.all_gather(payload, "pb", axis=0)
    coeff_all = got[:, :panel].reshape(npb, ncore, half, own_items)
    contract = (((0, 1), (0, 1)), ((), ()))
    item_grads = lax.dot_general(
        coeff_all[:, my_core], q_half, contract, preferred_element_type=jnp.float32
    ) + lax.dot_general(
        coeff_all[:, 1 - my_core], other_half, contract, preferred_element_type=jnp.float32
    )
    qg_parts, item_grads = lax.optimization_barrier((qg_parts, item_grads))
    question_grads = jnp.sum(qg_parts, axis=0)
    loss_parts = got[:, panel, :3].astype(jnp.float32)
    total = jnp.sum(loss_parts[:, 0] + loss_parts[:, 1] + loss_parts[:, 2])
    loss = total / (panel * npb)
    return (loss, question_grads, item_grads)


def solution(mesh):
    npb, nitem = mesh.devices.shape
    ncore = 2
    nz = 8 if nitem % (8 * ncore) == 0 else 1
    fine = Mesh(mesh.devices.reshape(npb, nitem // (nz * ncore), nz, ncore), ("pb",) + ITEM)
    qspec = ("pb",) + ITEM
    return jax.shard_map(
        shards,
        mesh=fine,
        in_specs=(
            P(qspec, None),
            P(ITEM, None),
            P(qspec, None),
            P(qspec, None, None),
        ),
        out_specs=(P(), P(qspec, None), P(ITEM, None)),
        check_vma=False,
    )
```

```python
import jax
import jax.numpy as jnp
from jax import lax
from jax.sharding import Mesh, PartitionSpec as P


ITEM = ("y", "z", "c")


def row_lse(values):
    top = jnp.max(values, axis=1)
    return top + jnp.log(jnp.sum(jnp.exp(values - top[:, None]), axis=1))


def bf16_pieces(x):
    hi = lax.reduce_precision(x, exponent_bits=8, mantissa_bits=7)
    rest = x - hi
    mid = lax.reduce_precision(rest, exponent_bits=8, mantissa_bits=7)
    lo = lax.reduce_precision(rest - mid, exponent_bits=8, mantissa_bits=7)
    return jnp.stack([hi, mid, lo], axis=-1)


def shards(questions, item_embeddings, block_ids, teacher_scores):
    qdev, width = questions.shape
    slots = block_ids.shape[1]
    blk = teacher_scores.shape[2]
    own_items = item_embeddings.shape[0]
    blocks_here = own_items // blk
    nitem = lax.axis_size(ITEM)
    nblk = nitem * blocks_here
    panel = qdev * nitem
    base = lax.axis_index(ITEM) * blocks_here

    named = block_ids[:, :, None] == jnp.arange(nblk, dtype=jnp.int32)[None, None, :]
    routed = jnp.einsum(
        "qjb,qjk->bqk",
        named.astype(jnp.bfloat16),
        teacher_scores,
        preferred_element_type=jnp.float32,
    ).astype(jnp.bfloat16)
    routed = routed.reshape(nitem, blocks_here, qdev, blk).transpose(0, 2, 1, 3)
    routed = routed.reshape(nitem, qdev, own_items)

    ncore = lax.axis_size("c")
    nchip = nitem // ncore
    mask = jnp.any(named, axis=1).astype(jnp.bfloat16).reshape(qdev, nchip, ncore * blocks_here)
    lse_own = bf16_pieces(row_lse(teacher_scores.astype(jnp.float32).reshape(qdev, slots * blk)))
    lse_own = lse_own.astype(jnp.bfloat16)
    nmask = ncore * blocks_here
    pad = -(-(nmask + 3) // 128) * 128 - nmask - 3
    tail = jnp.concatenate(
        [
            mask.transpose(1, 0, 2),
            jnp.broadcast_to(lse_own[None], (nchip, qdev, 3)),
            jnp.zeros((nchip, qdev, pad), jnp.bfloat16),
        ],
        axis=2,
    )
    routed = routed.reshape(nchip, ncore, qdev, own_items).transpose(0, 2, 1, 3)
    routed = routed.reshape(nchip, qdev, ncore * own_items)
    send = jnp.concatenate(
        [jnp.broadcast_to(questions[None], (nchip, qdev, width)), routed, tail], axis=2
    )
    recv = lax.all_to_all(send, ("y", "z"), 0, 0, tiled=False)
    per_core = []
    for core in range(ncore):
        t0 = width + core * own_items
        per_core.append(
            jnp.concatenate(
                [
                    recv[:, :, :width],
                    recv[:, :, t0 : t0 + own_items],
                    recv[:, :, width + ncore * own_items :],
                ],
                axis=2,
            )
        )
    recv = lax.all_to_all(jnp.stack(per_core), "c", 0, 0, tiled=False)
    recv = recv.transpose(1, 0, 2, 3).reshape(panel, -1)
    my_core = lax.axis_index("c")
    gathered_q = recv[:, :width]
    teach_local = recv[:, width : width + own_items]
    teach_local = teach_local.reshape(panel, blocks_here, blk).astype(jnp.float32)
    tail0 = width + own_items
    valid = lax.dynamic_slice_in_dim(recv, tail0 + my_core * blocks_here, blocks_here, axis=1)
    valid = (valid > 0.5)[:, :, None]
    lse_parts = recv[:, tail0 + nmask : tail0 + nmask + 3]
    lse_parts = lse_parts.astype(jnp.float32)
    lse_t = lse_parts[:, 0] + lse_parts[:, 1] + lse_parts[:, 2]
    half = panel // ncore
    q_half = lax.all_gather(
        lax.dynamic_slice_in_dim(gathered_q, my_core * half, half, axis=0), "pb", axis=0
    )

    scores = lax.dot_general(
        gathered_q, item_embeddings, (((1,), (1,)), ((), ())), preferred_element_type=jnp.float32
    ).reshape(panel, blocks_here, blk)
    target = jnp.exp(teach_local - lse_t[:, None, None])

    masked = jnp.where(valid, scores, -jnp.inf)
    m_part = jnp.max(masked, axis=(1, 2))
    l_part = jnp.sum(jnp.where(valid, jnp.exp(scores - m_part[:, None, None]), 0.0), axis=(1, 2))
    d_part = jnp.sum(jnp.where(valid, target * (teach_local - scores), 0.0), axis=(1, 2))
    stacked = jnp.stack([m_part, l_part, d_part])
    parts = lax.all_to_all(
        jnp.broadcast_to(stacked[None], (nchip,) + stacked.shape), ("y", "z"), 0, 0, tiled=False
    )
    other = lax.ppermute(parts, "c", [(0, 1), (1, 0)])
    parts = jnp.where(my_core == 0, jnp.stack([parts, other]), jnp.stack([other, parts]))
    parts = parts.reshape((nitem,) + stacked.shape)
    m_all, l_all, d_all = parts[:, 0], parts[:, 1], parts[:, 2]
    m_s = jnp.max(m_all, axis=0)
    lse_s = m_s + jnp.log(jnp.sum(l_all * jnp.exp(m_all - m_s[None, :]), axis=0))
    row_loss = jnp.sum(jnp.sum(d_all, axis=0) - lse_t + lse_s)

    probs = jnp.exp(scores - lse_s[:, None, None])
    coeff = jnp.where(valid, probs - target, 0.0).astype(jnp.bfloat16)
    dense_rows = coeff.reshape(panel, own_items)

    qg = jnp.dot(dense_rows, item_embeddings, preferred_element_type=jnp.float32)
    qg = qg.reshape(nchip, ncore, qdev, width).transpose(1, 0, 2, 3)
    qg = jnp.sum(lax.all_to_all(qg, "c", 0, 0, tiled=False), axis=0)
    qg_parts = lax.all_to_all(qg, ("y", "z"), 0, 0, tiled=False)
    npb = lax.axis_size("pb")
    pieces = jnp.zeros((8, own_items), jnp.float32).at[0, :3].set(bf16_pieces(row_loss))
    payload = jnp.concatenate([dense_rows, pieces.astype(jnp.bfloat16)], axis=0)
    payload, q_half = lax.optimization_barrier((payload, q_half))
    other_half = lax.ppermute(q_half, "c", [(0, 1), (1, 0)])
    got = lax.all_gather(payload, "pb", axis=0)
    coeff_all = got[:, :panel].reshape(npb, ncore, half, own_items)
    contract = (((0, 1), (0, 1)), ((), ()))
    item_grads = lax.dot_general(
        coeff_all[:, my_core], q_half, contract, preferred_element_type=jnp.float32
    ) + lax.dot_general(
        coeff_all[:, 1 - my_core], other_half, contract, preferred_element_type=jnp.float32
    )
    qg_parts, item_grads = lax.optimization_barrier((qg_parts, item_grads))
    question_grads = jnp.sum(qg_parts, axis=0)
    loss_parts = got[:, panel, :3].astype(jnp.float32)
    total = jnp.sum(loss_parts[:, 0] + loss_parts[:, 1] + loss_parts[:, 2])
    loss = total / (panel * npb)
    return (loss, question_grads, item_grads)


def solution(mesh):
    npb, nitem = mesh.devices.shape
    ncore = 2
    nz = 8 if nitem % (8 * ncore) == 0 else 1
    fine = Mesh(mesh.devices.reshape(npb, nitem // (nz * ncore), nz, ncore), ("pb",) + ITEM)
    qspec = ("pb",) + ITEM
    return jax.shard_map(
        shards,
        mesh=fine,
        in_specs=(
            P(qspec, None),
            P(ITEM, None),
            P(qspec, None),
            P(qspec, None, None),
        ),
        out_specs=(P(), P(qspec, None), P(ITEM, None)),
        check_vma=False,
    )
```

```python
import jax
import jax.numpy as jnp
from jax import lax
from jax.sharding import Mesh, PartitionSpec as P


ITEM = ("y", "z", "c")


def row_lse(values):
    top = jnp.max(values, axis=1)
    return top + jnp.log(jnp.sum(jnp.exp(values - top[:, None]), axis=1))


def bf16_pieces(x):
    hi = lax.reduce_precision(x, exponent_bits=8, mantissa_bits=7)
    rest = x - hi
    mid = lax.reduce_precision(rest, exponent_bits=8, mantissa_bits=7)
    lo = lax.reduce_precision(rest - mid, exponent_bits=8, mantissa_bits=7)
    return jnp.stack([hi, mid, lo], axis=-1)


def shards(questions, item_embeddings, block_ids, teacher_scores):
    qdev, width = questions.shape
    slots = block_ids.shape[1]
    blk = teacher_scores.shape[2]
    own_items = item_embeddings.shape[0]
    blocks_here = own_items // blk
    nitem = lax.axis_size(ITEM)
    nblk = nitem * blocks_here
    panel = qdev * nitem
    base = lax.axis_index(ITEM) * blocks_here

    named = block_ids[:, :, None] == jnp.arange(nblk, dtype=jnp.int32)[None, None, :]
    routed = jnp.einsum(
        "qjb,qjk->bqk",
        named.astype(jnp.bfloat16),
        teacher_scores,
        preferred_element_type=jnp.float32,
    ).astype(jnp.bfloat16)
    routed = routed.reshape(nitem, blocks_here, qdev, blk).transpose(0, 2, 1, 3)
    routed = routed.reshape(nitem, qdev, own_items)

    ncore = lax.axis_size("c")
    nchip = nitem // ncore
    mask = jnp.any(named, axis=1).astype(jnp.bfloat16).reshape(qdev, nchip, ncore * blocks_here)
    lse_own = bf16_pieces(row_lse(teacher_scores.astype(jnp.float32).reshape(qdev, slots * blk)))
    lse_own = lse_own.astype(jnp.bfloat16)
    nmask = ncore * blocks_here
    pad = -(-(nmask + 3) // 128) * 128 - nmask - 3
    tail = jnp.concatenate(
        [
            mask.transpose(1, 0, 2),
            jnp.broadcast_to(lse_own[None], (nchip, qdev, 3)),
            jnp.zeros((nchip, qdev, pad), jnp.bfloat16),
        ],
        axis=2,
    )
    routed = routed.reshape(nchip, ncore, qdev, own_items).transpose(0, 2, 1, 3)
    routed = routed.reshape(nchip, qdev, ncore * own_items)
    send = jnp.concatenate(
        [jnp.broadcast_to(questions[None], (nchip, qdev, width)), routed, tail], axis=2
    )
    recv = lax.all_to_all(send, ("y", "z"), 0, 0, tiled=False)
    my_core = lax.axis_index("c")

    def for_core(core):
        return jnp.concatenate(
            [
                recv[:, :, :width],
                lax.dynamic_slice_in_dim(recv, width + core * own_items, own_items, axis=2),
                recv[:, :, width + ncore * own_items :],
            ],
            axis=2,
        )

    mine = for_core(my_core)
    other = lax.ppermute(for_core(1 - my_core), "c", [(0, 1), (1, 0)])
    recv = jnp.where(my_core == 0, jnp.stack([mine, other], 1), jnp.stack([other, mine], 1))
    recv = recv.reshape(panel, -1)
    gathered_q = recv[:, :width]
    teach_local = recv[:, width : width + own_items]
    teach_local = teach_local.reshape(panel, blocks_here, blk).astype(jnp.float32)
    tail0 = width + own_items
    valid = lax.dynamic_slice_in_dim(recv, tail0 + my_core * blocks_here, blocks_here, axis=1)
    valid = (valid > 0.5)[:, :, None]
    lse_parts = recv[:, tail0 + nmask : tail0 + nmask + 3]
    lse_parts = lse_parts.astype(jnp.float32)
    lse_t = lse_parts[:, 0] + lse_parts[:, 1] + lse_parts[:, 2]
    half = panel // ncore
    q_half = lax.all_gather(
        lax.dynamic_slice_in_dim(gathered_q, my_core * half, half, axis=0), "pb", axis=0
    )

    scores = lax.dot_general(
        gathered_q, item_embeddings, (((1,), (1,)), ((), ())), preferred_element_type=jnp.float32
    ).reshape(panel, blocks_here, blk)
    target = jnp.exp(teach_local - lse_t[:, None, None])

    masked = jnp.where(valid, scores, -jnp.inf)
    m_part = jnp.max(masked, axis=(1, 2))
    l_part = jnp.sum(jnp.where(valid, jnp.exp(scores - m_part[:, None, None]), 0.0), axis=(1, 2))
    d_part = jnp.sum(jnp.where(valid, target * (teach_local - scores), 0.0), axis=(1, 2))
    stacked = jnp.stack([m_part, l_part, d_part])
    parts = lax.all_to_all(
        jnp.broadcast_to(stacked[None], (nchip,) + stacked.shape), ("y", "z"), 0, 0, tiled=False
    )
    other = lax.ppermute(parts, "c", [(0, 1), (1, 0)])
    parts = jnp.where(my_core == 0, jnp.stack([parts, other]), jnp.stack([other, parts]))
    parts = parts.reshape((nitem,) + stacked.shape)
    m_all, l_all, d_all = parts[:, 0], parts[:, 1], parts[:, 2]
    m_s = jnp.max(m_all, axis=0)
    lse_s = m_s + jnp.log(jnp.sum(l_all * jnp.exp(m_all - m_s[None, :]), axis=0))
    row_loss = jnp.sum(jnp.sum(d_all, axis=0) - lse_t + lse_s)

    probs = jnp.exp(scores - lse_s[:, None, None])
    coeff = jnp.where(valid, probs - target, 0.0).astype(jnp.bfloat16)
    dense_rows = coeff.reshape(panel, own_items)

    qg = jnp.dot(dense_rows, item_embeddings, preferred_element_type=jnp.float32)
    qg = qg.reshape(nchip, ncore, qdev, width).transpose(1, 0, 2, 3)
    qg = jnp.sum(lax.all_to_all(qg, "c", 0, 0, tiled=False), axis=0)
    qg_parts = lax.all_to_all(qg, ("y", "z"), 0, 0, tiled=False)
    npb = lax.axis_size("pb")
    pieces = jnp.zeros((8, own_items), jnp.float32).at[0, :3].set(bf16_pieces(row_loss))
    payload = jnp.concatenate([dense_rows, pieces.astype(jnp.bfloat16)], axis=0)
    payload, q_half = lax.optimization_barrier((payload, q_half))
    other_half = lax.ppermute(q_half, "c", [(0, 1), (1, 0)])
    got = lax.all_gather(payload, "pb", axis=0)
    coeff_all = got[:, :panel].reshape(npb, ncore, half, own_items)
    contract = (((0, 1), (0, 1)), ((), ()))
    item_grads = lax.dot_general(
        coeff_all[:, my_core], q_half, contract, preferred_element_type=jnp.float32
    ) + lax.dot_general(
        coeff_all[:, 1 - my_core], other_half, contract, preferred_element_type=jnp.float32
    )
    qg_parts, item_grads = lax.optimization_barrier((qg_parts, item_grads))
    question_grads = jnp.sum(qg_parts, axis=0)
    loss_parts = got[:, panel, :3].astype(jnp.float32)
    total = jnp.sum(loss_parts[:, 0] + loss_parts[:, 1] + loss_parts[:, 2])
    loss = total / (panel * npb)
    return (loss, question_grads, item_grads)


def solution(mesh):
    npb, nitem = mesh.devices.shape
    ncore = 2
    nz = 8 if nitem % (8 * ncore) == 0 else 1
    fine = Mesh(mesh.devices.reshape(npb, nitem // (nz * ncore), nz, ncore), ("pb",) + ITEM)
    qspec = ("pb",) + ITEM
    return jax.shard_map(
        shards,
        mesh=fine,
        in_specs=(
            P(qspec, None),
            P(ITEM, None),
            P(qspec, None),
            P(qspec, None, None),
        ),
        out_specs=(P(), P(qspec, None), P(ITEM, None)),
        check_vma=False,
    )
```
